256 devices in a mesh: px: 8 (over y, core), py: 32 (over x, z).
Axes of the slice: x: 4, y: 4, z: 8, core: 2. Of those that a mesh axis runs over, the one named last changes fastest.
Arguments:
- prim_elem: bfloat16 [80, 524288], P(None, ('px', 'py')), may hold values from -6 to 6
- forcing: bfloat16 [140, 524288], P(None, ('px', 'py')), may hold values from -6 to 6
- adj_source: bfloat16 [140, 524288], P(None, ('px', 'py')), may hold values from -6 to 6
- elem_volume: float32 [524288], P(('px', 'py')), may hold values from 0.25 to 12, as said below
- face_link: int32 [4, 524288], P(None, ('px', 'py')), may hold values from 0 to 11648, as said below
- send_map: int32 [256, 3456], P(('px', 'py')), may hold values from 0 to 8192, as said below
- elem_count: int32 [256], P(('px', 'py')), may hold values from 1024 to 2048, as said below
- prolong_elem: bfloat16 [140, 80], replicated, may hold values from -0.625 to 0.625
- face_trace: bfloat16 [4, 40, 80], replicated, may hold values from -0.625 to 0.625
- prolong_face: bfloat16 [60, 40], replicated, may hold values from -1 to 1
- stiffness: bfloat16 [140, 140], replicated, may hold values from -0.5 to 0.5
- conv_grad: bfloat16 [140, 140], replicated, may hold values from -0.5 to 0.5
- conv_out: bfloat16 [140, 140], replicated, may hold values from -0.5 to 0.5
- lift: bfloat16 [140, 4, 60], replicated, may hold values from -0.375 to 0.375
- adj_trace: bfloat16 [4, 60, 140], replicated, may hold values from -0.5 to 0.5
- adj_lift: bfloat16 [140, 4, 60], replicated, may hold values from -0.25 to 0.25
- block_corr: bfloat16 [140, 140], replicated, may hold values from -0.25 to 0.25
Outputs:
- indicator_share: float32 [524288], P(('px', 'py'))
- mean_error: float32 [1], replicated
The draws below stay inside these ranges and needn't reach their ends.
Inputs may be any that keep to these rules, and one draw needn't show every extreme that they name: `face_link`: entries below 8192 name a local face of the same device; an entry 8192 + q*384 + s names slot s from the partition at offset q; the largest value marks a boundary face. Links are mutual: a local link's target links back, and device d's slot s toward offset q holds the face whose link names slot s from offset q exactly when the partition at offset q uses its slot s toward offset 8 - q. Faces of elements at or beyond the device's count are boundary faces. `send_map`: row d, entry q*384 + s is the local face of device d sent in slot s toward offset q, or 8192 for an unused slot; used faces are distinct and belong to live elements; slots toward offset 4 (the device itself) and toward offsets outside the grid are unused. `elem_count`: live elements of a device occupy its first local columns; some device is full and some device holds exactly the least. `elem_volume`: positive element volumes.
All inputs are finite; a program needn't handle non-finite values.
Results may differ from the reference program's by a relative error of at most 0.0055.
Values may be sent and summed in bfloat16 or wider, within the bound.
No kernel may reach another device: no remote copies, remote signals or barrier semaphores. Data moves between devices by JAX's collectives and lax.ppermute only.
A program may use at most 64 MiB of HBM per device.

```python
import math
import jax
import jax.numpy as jnp
from jax import lax

NV = 140
NC = 80
NFV = 60
NFC = 40
SLOTS = 384
SWEEPS = 2
E_DEV = 2048
NEL = 524288
N_PX = 8
N_PY = 32


def build_links(key):
    devices = N_PX * N_PY
    base = jax.random.fold_in(key, 11)
    keys = jax.random.split(base, 6)
    faces = 4 * E_DEV
    slot_total = 9 * SLOTS
    dropped = jax.random.randint(keys[0], (devices,), 0, E_DEV // 2 + 1)
    fullest = jax.random.randint(keys[1], (), 0, devices)
    thinnest = (fullest + 1) % devices
    dropped = jnp.where(jnp.arange(devices) == thinnest, E_DEV // 2, dropped)
    dropped = jnp.where(jnp.arange(devices) == fullest, 0, dropped)
    counts = (E_DEV - dropped).astype(jnp.int32)
    bits = jax.random.randint(keys[2], (devices, 9, SLOTS), 0, 4) != 0
    device_ids = jnp.arange(devices)
    grid_row = device_ids // N_PY
    grid_col = device_ids % N_PY
    offsets = jnp.arange(9)
    near_row = grid_row[:, None] + offsets[None, :] // 3 - 1
    near_col = grid_col[:, None] + offsets[None, :] % 3 - 1
    exists = (near_row >= 0) & (near_row < N_PX) & (near_col >= 0) & (near_col < N_PY) & (offsets[None, :] != 4)
    peer = jnp.clip(near_row, 0, N_PX - 1) * N_PY + jnp.clip(near_col, 0, N_PY - 1)
    lanes = jnp.arange(SLOTS)[None, None, :]
    mirrored = bits[peer[:, :, None], (8 - offsets)[None, :, None], lanes]
    paired = jnp.where(offsets[None, :, None] < 4, bits, mirrored)
    active = (paired & exists[:, :, None]).reshape(devices, slot_total)
    face_ids = jnp.arange(faces)
    valid = face_ids[None, :] % E_DEV < counts[:, None]
    scores = jax.random.randint(keys[3], (devices, faces), 0, 1 << 20)
    order = jnp.argsort(jnp.where(valid, scores, 1 << 21), axis=1, stable=True)
    chosen = order[:, :slot_total]
    device_rows = jnp.arange(devices)[:, None]
    remote = jnp.zeros((devices, faces), jnp.int32).at[device_rows, chosen].max(active.astype(jnp.int32))
    spare = valid & (remote == 0)
    scores_two = jax.random.randint(keys[4], (devices, faces), 0, 1 << 20)
    order_two = jnp.argsort(jnp.where(spare, scores_two, 1 << 21), axis=1, stable=True)
    spare_count = jnp.sum(spare.astype(jnp.int32), axis=1)
    position = jnp.arange(faces)
    partner_pos = jnp.bitwise_xor(position, 1)
    boundary_bits = jax.random.randint(keys[5], (devices, faces // 2), 0, 8) == 0
    boundary = boundary_bits[:, position // 2] | (position[None, :] // 2 == 0)
    linked = (jnp.bitwise_or(position, 1)[None, :] < spare_count[:, None]) & jnp.logical_not(boundary)
    sentinel = faces + slot_total
    values = jnp.where(linked, order_two[:, partner_pos], sentinel).astype(jnp.int32)
    link = jnp.full((devices, faces), sentinel, jnp.int32).at[device_rows, order_two].set(values)
    slot_index = (faces + jnp.arange(slot_total)).astype(jnp.int32)
    current = jnp.take_along_axis(link, chosen, axis=1)
    link = link.at[device_rows, chosen].set(jnp.where(active, slot_index[None, :], current))
    send_rows = jnp.where(active, chosen, faces).astype(jnp.int32)
    face_link = link.reshape(devices, 4, E_DEV).transpose(1, 0, 2).reshape(4, devices * E_DEV)
    return (face_link.astype(jnp.int32), send_rows, counts)


def draw_face_link(key, part):
    return build_links(key)[0]


def draw_send_map(key, part):
    return build_links(key)[1]


def draw_elem_count(key, part):
    return build_links(key)[2]


def draw_elem_volume(key, part):
    devices = N_PX * N_PY
    base = jax.random.fold_in(key, 23)
    owner = (jnp.arange(devices * E_DEV) // E_DEV).astype(jnp.float32)
    ramp = 1.0 + 2.0 * owner / max(devices - 1, 1)
    spread = jnp.exp(jax.random.uniform(base, (devices * E_DEV,), jnp.float32, math.log(0.25), math.log(4.0)))
    return (ramp * spread).astype(jnp.float32)


def level_of(rng, extent, cuts, low, top_value):
    gain, own = 1.0, jax.random.fold_in(rng, 6)
    for dim, parts in cuts:
        heights = jnp.exp(jax.random.uniform(jax.random.fold_in(own, dim), (parts,), jnp.float32, low / len(cuts), top_value / len(cuts)))
        gain = gain * jnp.repeat(heights, extent[dim] // parts).reshape([-1 if axis == dim else 1 for axis in range(len(extent))])
    return gain


def gaussian(own_key, dims, scale, most, shards=(), kind=jnp.bfloat16):
    entries = jax.random.normal(own_key, dims, jnp.float32) * scale
    if len(shards) > 0:
        entries = level_of(own_key, dims, shards, -0.22, 0.18) * entries
    return jnp.clip(entries, min=-most, max=most).astype(kind)


def setup_inputs(seed: int = 0) -> dict:
    key_list = jax.random.split(jax.random.key(seed), 18)
    return {
        "prim_elem": gaussian(key_list[0], (NC, NEL), 1.0, 6.0, ((1, 256),)),
        "forcing": gaussian(key_list[1], (NV, NEL), 1.0, 6.0, ((1, 256),)),
        "adj_source": gaussian(key_list[2], (NV, NEL), 1.0, 6.0, ((1, 256),)),
        "elem_volume": draw_elem_volume(jax.random.fold_in(key_list[17], 71), 0),
        "face_link": draw_face_link(jax.random.fold_in(key_list[17], 71), 0),
        "send_map": draw_send_map(jax.random.fold_in(key_list[17], 71), 0),
        "elem_count": draw_elem_count(jax.random.fold_in(key_list[17], 71), 0),
        "prolong_elem": gaussian(key_list[7], (NV, NC), NC ** -0.5, 0.625),
        "face_trace": gaussian(key_list[8], (4, NFC, NC), NC ** -0.5, 0.625),
        "prolong_face": gaussian(key_list[9], (NFV, NFC), NFC ** -0.5, 1.0),
        "stiffness": gaussian(key_list[10], (NV, NV), NV ** -0.5, 0.5),
        "conv_grad": gaussian(key_list[11], (NV, NV), NV ** -0.5, 0.5),
        "conv_out": gaussian(key_list[12], (NV, NV), NV ** -0.5, 0.5),
        "lift": gaussian(key_list[13], (NV, 4, NFV), (4 * NFV) ** -0.5, 0.375),
        "adj_trace": gaussian(key_list[14], (4, NFV, NV), NV ** -0.5, 0.5),
        "adj_lift": gaussian(key_list[15], (NV, 4, NFV), (8 * NFV) ** -0.5, 0.25),
        "block_corr": gaussian(key_list[16], (NV, NV), (4 * NV) ** -0.5, 0.25),
    }


def to_half(value):
    return lax.optimization_barrier(value.astype(jnp.bfloat16))


def wide(value):
    return value.astype(jnp.float32)


def by_device(array, devices):
    height = array.shape[0]
    return array.reshape(height, devices, -1).transpose(1, 0, 2)


def gather_faces(own_vals, received, face_link):
    height = own_vals.shape[0]
    columns = jnp.concatenate([own_vals.reshape(height, -1), received], axis=1)
    picked = jnp.take(columns, face_link.reshape(-1).astype(jnp.int32), axis=1, mode="fill", fill_value=0)
    return picked.reshape(height, 4, -1)


def outgoing(own_vals, slot_row):
    height = own_vals.shape[0]
    return jnp.take(own_vals.reshape(height, -1), slot_row.astype(jnp.int32), axis=1, mode="fill", fill_value=0)


def swap_slots(parcels):
    height = parcels.shape[1]
    grid = parcels.reshape(N_PX, N_PY, height, 3, 3, SLOTS)
    padded = jnp.pad(grid, ((1, 1), (1, 1), (0, 0), (0, 0), (0, 0), (0, 0)))
    stacked_rows = []
    for row_pick in range(3):
        stacked_cols = []
        for col_pick in range(3):
            stacked_cols.append(padded[row_pick:row_pick + N_PX, col_pick:col_pick + N_PY, :, 2 - row_pick, 2 - col_pick, :])
        stacked_rows.append(jnp.stack(stacked_cols, axis=3))
    moved = jnp.stack(stacked_rows, axis=3)
    return moved.reshape(N_PX * N_PY, height, 9 * SLOTS)


def block_step(right_side, block_corr):
    return right_side + jnp.dot(block_corr, to_half(right_side), preferred_element_type=jnp.float32)


def adjoint_faces(adjoint, adj_trace):
    return to_half(jnp.einsum("jrv,ve->rje", wide(adj_trace), wide(to_half(adjoint))))


def adjoint_chain(adj_one, link_one, received_list, adj_trace, adj_lift, block_corr):
    source = wide(adj_one)
    adjoint = block_step(source, block_corr)
    for received in received_list:
        face_vals = adjoint_faces(adjoint, adj_trace)
        partner = gather_faces(face_vals, received, link_one)
        coupling = jnp.einsum("vjr,rje->ve", wide(adj_lift), wide(partner))
        adjoint = block_step(source - coupling, block_corr)
    return adjoint


def primal_trace(prim_one, face_trace, prolong_face):
    coarse = to_half(jnp.einsum("jrc,ce->rje", wide(face_trace), wide(prim_one)))
    return jnp.einsum("fr,rje->fje", wide(prolong_face), wide(coarse))


def reference(prim_elem, forcing, adj_source, elem_volume, face_link, send_map, elem_count, prolong_elem, face_trace, prolong_face, stiffness, conv_grad, conv_out, lift, adj_trace, adj_lift, block_corr):
    devices = N_PX * N_PY
    prim_dev = by_device(prim_elem, devices)
    force_dev = by_device(forcing, devices)
    source_dev = by_device(adj_source, devices)
    link_dev = by_device(face_link, devices)
    volume_dev = elem_volume.reshape(devices, -1)
    received_list = []
    for sweep_index in range(SWEEPS):
        def send_adjoint(inputs):
            adjoint = adjoint_chain(inputs[0], inputs[1], list(inputs[3:]), adj_trace, adj_lift, block_corr)
            return outgoing(adjoint_faces(adjoint, adj_trace), inputs[2])

        parcels = lax.map(send_adjoint, (source_dev, link_dev, send_map) + tuple(received_list))
        received_list.append(swap_slots(parcels))

    def send_primal(inputs):
        return outgoing(primal_trace(inputs[0], face_trace, prolong_face), inputs[1])

    primal_recv = swap_slots(lax.map(send_primal, (prim_dev, send_map)))

    def finish(inputs):
        prim_one, force_one, adj_one, link_one, volume_one, count_one, primal_one = inputs[:7]
        adjoint = adjoint_chain(adj_one, link_one, list(inputs[7:]), adj_trace, adj_lift, block_corr)
        own_trace = primal_trace(prim_one, face_trace, prolong_face)
        state_elem = to_half(jnp.dot(prolong_elem, prim_one, preferred_element_type=jnp.float32))
        conv_in = jnp.dot(conv_grad, state_elem, preferred_element_type=jnp.float32)
        conv_flux = to_half(wide(state_elem) * conv_in)
        neighbour = gather_faces(own_trace, primal_one, link_one)
        trace_jump = to_half(own_trace - neighbour)
        residual = jnp.dot(stiffness, state_elem, preferred_element_type=jnp.float32)
        residual = residual + jnp.dot(conv_out, conv_flux, preferred_element_type=jnp.float32)
        residual = residual + jnp.einsum("vjr,rje->ve", wide(lift), wide(trace_jump)) - wide(force_one)
        measure = jnp.abs(jnp.sum(adjoint * residual, axis=0))
        alive = jnp.arange(measure.shape[0]) < count_one
        return jnp.where(alive, volume_one * measure, jnp.zeros_like(measure))

    weighted = lax.map(finish, (prim_dev, force_dev, source_dev, link_dev, volume_dev, elem_count, primal_recv) + tuple(received_list))
    error_sum = jnp.sum(weighted)
    live_count = jnp.sum(wide(elem_count))
    mean_error = error_sum / live_count
    return (weighted / mean_error).reshape(-1), jnp.reshape(mean_error, (1,))
```

```python
import jax
import jax.numpy as jnp
from jax import lax
from jax.sharding import PartitionSpec as P

SWEEPS = 2
AXES = ("px", "py")


def take_rows(rows, index):
    return jnp.take(rows, index, axis=0, mode="fill", fill_value=0)


def exchange(parcel):
    n_px = lax.axis_size("px")
    n_py = lax.axis_size("py")
    blocks = [None] * 9
    for q in range(9):
        if q == 4:
            continue
        da, db = q // 3 - 1, q % 3 - 1
        pairs = []
        for r in range(n_px):
            for c in range(n_py):
                rr, cc = r + da, c + db
                if 0 <= rr < n_px and 0 <= cc < n_py:
                    pairs.append((r * n_py + c, rr * n_py + cc))
        blocks[8 - q] = lax.ppermute(parcel[q], AXES, pairs)
    blocks[4] = jnp.zeros_like(parcel[4])
    return jnp.concatenate(blocks, axis=0)


def local(
    prim_elem,
    forcing,
    adj_source,
    elem_volume,
    face_link,
    send_map,
    elem_count,
    prolong_elem,
    face_trace,
    prolong_face,
    stiffness,
    conv_grad,
    conv_out,
    lift,
    adj_trace,
    adj_lift,
    block_corr,
):
    elems = face_link.shape[1]
    face_total = 4 * elems
    slot_total = send_map.shape[1]
    src_total = face_total + slot_total
    slot_row = jnp.clip(send_map[0], 0, face_total)
    link = jnp.clip(face_link.reshape(-1), 0, src_total)
    width = prolong_face.shape[0]

    coarse = jnp.einsum(
        "jrc,ce->jer", face_trace, prim_elem, preferred_element_type=jnp.float32
    ).astype(jnp.bfloat16)
    own_trace = jnp.einsum("jer,fr->jef", coarse, prolong_face, preferred_element_type=jnp.float32)
    own_rows = own_trace.reshape(face_total, -1)

    source = adj_source.astype(jnp.float32)
    adjoint = source + jnp.dot(block_corr, adj_source, preferred_element_type=jnp.float32)

    def adj_faces(adjoint):
        face_vals = jnp.einsum(
            "jrv,ve->jer",
            adj_trace,
            adjoint.astype(jnp.bfloat16),
            preferred_element_type=jnp.float32,
        ).astype(jnp.bfloat16)
        return face_vals.reshape(face_total, -1)

    def sweep_tail(partner, adjoint_unused=None):
        coupling = jnp.einsum(
            "vjr,jer->ve", adj_lift, partner.reshape(4, elems, -1), preferred_element_type=jnp.float32
        )
        right_side = source - coupling
        return right_side + jnp.dot(
            block_corr, right_side.astype(jnp.bfloat16), preferred_element_type=jnp.float32
        )

    zero_row = lambda w: jnp.zeros((1, w), jnp.float32)

    face_rows = adj_faces(adjoint)
    both = jnp.concatenate([own_rows, face_rows.astype(jnp.float32)], axis=1)
    both_pad = jnp.concatenate([both, zero_row(2 * width)], axis=0)
    parcel = take_rows(both_pad, slot_row).astype(jnp.bfloat16)
    received = exchange(parcel.reshape(9, -1, 2 * width)).astype(jnp.float32)
    pool = jnp.concatenate([both, received, zero_row(2 * width)], axis=0)
    picked = take_rows(pool, link)
    neighbour = picked[:, :width]
    partner = picked[:, width:].astype(jnp.bfloat16)
    adjoint = sweep_tail(partner)

    for sweep_index in range(1, SWEEPS):
        face_rows = adj_faces(adjoint).astype(jnp.float32)
        face_pad = jnp.concatenate([face_rows, zero_row(width)], axis=0)
        parcel = take_rows(face_pad, slot_row).astype(jnp.bfloat16)
        received = exchange(parcel.reshape(9, -1, width)).astype(jnp.float32)
        pool = jnp.concatenate([face_rows, received, zero_row(width)], axis=0)
        partner = take_rows(pool, link).astype(jnp.bfloat16)
        adjoint = sweep_tail(partner)

    state_elem = jnp.dot(prolong_elem, prim_elem, preferred_element_type=jnp.float32).astype(
        jnp.bfloat16
    )
    conv_in = jnp.dot(conv_grad, state_elem, preferred_element_type=jnp.float32)
    conv_flux = (state_elem * conv_in).astype(jnp.bfloat16)
    trace_jump = (own_rows - neighbour).astype(jnp.bfloat16).reshape(4, elems, -1)
    residual = jnp.dot(stiffness, state_elem, preferred_element_type=jnp.float32)
    residual = residual + jnp.dot(conv_out, conv_flux, preferred_element_type=jnp.float32)
    residual = (
        residual
        + jnp.einsum("vjr,jer->ve", lift, trace_jump, preferred_element_type=jnp.float32)
        - forcing.astype(jnp.float32)
    )
    measure = jnp.abs(jnp.sum(adjoint * residual, axis=0))
    alive = jnp.arange(measure.shape[0]) < elem_count[0]
    weighted = jnp.where(alive, elem_volume * measure, 0.0)
    totals = lax.psum(
        jnp.stack([jnp.sum(weighted), elem_count[0].astype(jnp.float32)]), AXES
    )
    mean_error = totals[0] / totals[1]
    return (weighted / mean_error, jnp.reshape(mean_error, (1,)))


def solution(mesh):
    placed = (
        P(None, AXES),
        P(None, AXES),
        P(None, AXES),
        P(AXES),
        P(None, AXES),
        P(AXES, None),
        P(AXES),
        P(),
        P(),
        P(),
        P(),
        P(),
        P(),
        P(),
        P(),
        P(),
        P(),
    )
    return jax.shard_map(
        local, mesh=mesh, in_specs=placed, out_specs=(P(AXES), P()), check_vma=False
    )
```

```python
import jax
import jax.numpy as jnp
from jax import lax
from jax.experimental import pallas as pl
from jax.experimental.pallas import tpu as pltpu
from jax.sharding import PartitionSpec as P

SWEEPS = 2
AXES = ("px", "py")


def _gather_kernel(idx_ref, src_ref, out_ref):
    def body(i, carry):
        row = idx_ref[i]
        out_ref[pl.ds(i, 1), :] = src_ref[pl.ds(row, 1), :]
        return carry

    lax.fori_loop(0, out_ref.shape[0], body, 0, unroll=16)


def take_rows(rows, index):
    count, width = index.shape[0], rows.shape[1]
    return pl.pallas_call(
        _gather_kernel,
        out_shape=jax.ShapeDtypeStruct((count, width), rows.dtype),
        in_specs=[
            pl.BlockSpec(memory_space=pltpu.SMEM),
            pl.BlockSpec(memory_space=pltpu.VMEM),
        ],
        out_specs=pl.BlockSpec(memory_space=pltpu.VMEM),
        cost_estimate=pl.CostEstimate(
            flops=0, transcendentals=0, bytes_accessed=2 * count * width * 4
        ),
    )(index, rows)


def exchange(parcel):
    n_px = lax.axis_size("px")
    n_py = lax.axis_size("py")
    blocks = [None] * 9
    for q in range(9):
        if q == 4:
            continue
        da, db = q // 3 - 1, q % 3 - 1
        pairs = []
        for r in range(n_px):
            for c in range(n_py):
                rr, cc = r + da, c + db
                if 0 <= rr < n_px and 0 <= cc < n_py:
                    pairs.append((r * n_py + c, rr * n_py + cc))
        blocks[8 - q] = lax.ppermute(parcel[q], AXES, pairs)
    blocks[4] = jnp.zeros_like(parcel[4])
    return jnp.concatenate(blocks, axis=0)


def local(
    prim_elem,
    forcing,
    adj_source,
    elem_volume,
    face_link,
    send_map,
    elem_count,
    prolong_elem,
    face_trace,
    prolong_face,
    stiffness,
    conv_grad,
    conv_out,
    lift,
    adj_trace,
    adj_lift,
    block_corr,
):
    elems = face_link.shape[1]
    face_total = 4 * elems
    slot_total = send_map.shape[1]
    src_total = face_total + slot_total
    slot_row = jnp.clip(send_map[0], 0, face_total)
    link = jnp.clip(face_link.reshape(-1), 0, src_total)
    width = prolong_face.shape[0]

    coarse = jnp.einsum(
        "jrc,ce->jer", face_trace, prim_elem, preferred_element_type=jnp.float32
    ).astype(jnp.bfloat16)
    own_trace = jnp.einsum("jer,fr->jef", coarse, prolong_face, preferred_element_type=jnp.float32)
    own_rows = own_trace.reshape(face_total, -1)

    source = adj_source.astype(jnp.float32)
    adjoint = source + jnp.dot(block_corr, adj_source, preferred_element_type=jnp.float32)

    def adj_faces(adjoint):
        face_vals = jnp.einsum(
            "jrv,ve->jer",
            adj_trace,
            adjoint.astype(jnp.bfloat16),
            preferred_element_type=jnp.float32,
        ).astype(jnp.bfloat16)
        return face_vals.reshape(face_total, -1)

    def sweep_tail(partner, adjoint_unused=None):
        coupling = jnp.einsum(
            "vjr,jer->ve", adj_lift, partner.reshape(4, elems, -1), preferred_element_type=jnp.float32
        )
        right_side = source - coupling
        return right_side + jnp.dot(
            block_corr, right_side.astype(jnp.bfloat16), preferred_element_type=jnp.float32
        )

    zero_row = lambda w: jnp.zeros((1, w), jnp.float32)

    face_rows = adj_faces(adjoint)
    both = jnp.concatenate([own_rows, face_rows.astype(jnp.float32)], axis=1)
    both_pad = jnp.concatenate([both, zero_row(2 * width)], axis=0)
    parcel = take_rows(both_pad, slot_row).astype(jnp.bfloat16)
    received = exchange(parcel.reshape(9, -1, 2 * width)).astype(jnp.float32)
    pool = jnp.concatenate([both, received, zero_row(2 * width)], axis=0)
    picked = take_rows(pool, link)
    neighbour = picked[:, :width]
    partner = picked[:, width:].astype(jnp.bfloat16)
    adjoint = sweep_tail(partner)

    for sweep_index in range(1, SWEEPS):
        face_rows = adj_faces(adjoint).astype(jnp.float32)
        face_pad = jnp.concatenate([face_rows, zero_row(width)], axis=0)
        parcel = take_rows(face_pad, slot_row).astype(jnp.bfloat16)
        received = exchange(parcel.reshape(9, -1, width)).astype(jnp.float32)
        pool = jnp.concatenate([face_rows, received, zero_row(width)], axis=0)
        partner = take_rows(pool, link).astype(jnp.bfloat16)
        adjoint = sweep_tail(partner)

    state_elem = jnp.dot(prolong_elem, prim_elem, preferred_element_type=jnp.float32).astype(
        jnp.bfloat16
    )
    conv_in = jnp.dot(conv_grad, state_elem, preferred_element_type=jnp.float32)
    conv_flux = (state_elem * conv_in).astype(jnp.bfloat16)
    trace_jump = (own_rows - neighbour).astype(jnp.bfloat16).reshape(4, elems, -1)
    residual = jnp.dot(stiffness, state_elem, preferred_element_type=jnp.float32)
    residual = residual + jnp.dot(conv_out, conv_flux, preferred_element_type=jnp.float32)
    residual = (
        residual
        + jnp.einsum("vjr,jer->ve", lift, trace_jump, preferred_element_type=jnp.float32)
        - forcing.astype(jnp.float32)
    )
    measure = jnp.abs(jnp.sum(adjoint * residual, axis=0))
    alive = jnp.arange(measure.shape[0]) < elem_count[0]
    weighted = jnp.where(alive, elem_volume * measure, 0.0)
    totals = lax.psum(
        jnp.stack([jnp.sum(weighted), elem_count[0].astype(jnp.float32)]), AXES
    )
    mean_error = totals[0] / totals[1]
    return (weighted / mean_error, jnp.reshape(mean_error, (1,)))


def solution(mesh):
    placed = (
        P(None, AXES),
        P(None, AXES),
        P(None, AXES),
        P(AXES),
        P(None, AXES),
        P(AXES, None),
        P(AXES),
        P(),
        P(),
        P(),
        P(),
        P(),
        P(),
        P(),
        P(),
        P(),
        P(),
    )
    return jax.shard_map(
        local, mesh=mesh, in_specs=placed, out_specs=(P(AXES), P()), check_vma=False
    )
```

```python
import jax
import jax.numpy as jnp
from jax import lax
from jax.experimental import pallas as pl
from jax.experimental.pallas import tpu as pltpu
from jax.sharding import PartitionSpec as P

SWEEPS = 2
AXES = ("px", "py")


def _gather_kernel(idx_ref, src_ref, out_ref):
    def body(i, carry):
        row = idx_ref[i]
        out_ref[pl.ds(i, 1), :] = src_ref[pl.ds(row, 1), :]
        return carry

    lax.fori_loop(0, out_ref.shape[0], body, 0, unroll=16)


def take_rows(rows, index):
    count, width = index.shape[0], rows.shape[1]
    return pl.pallas_call(
        _gather_kernel,
        out_shape=jax.ShapeDtypeStruct((count, width), rows.dtype),
        in_specs=[
            pl.BlockSpec(memory_space=pltpu.SMEM),
            pl.BlockSpec(memory_space=pltpu.VMEM),
        ],
        out_specs=pl.BlockSpec(memory_space=pltpu.VMEM),
        cost_estimate=pl.CostEstimate(
            flops=0, transcendentals=0, bytes_accessed=2 * count * width * 4
        ),
    )(index, rows)


def exchange(parcel):
    n_px = lax.axis_size("px")
    n_py = lax.axis_size("py")
    blocks = [None] * 9
    for q in range(9):
        if q == 4:
            continue
        da, db = q // 3 - 1, q % 3 - 1
        pairs = []
        for r in range(n_px):
            for c in range(n_py):
                rr, cc = r + da, c + db
                if 0 <= rr < n_px and 0 <= cc < n_py:
                    pairs.append((r * n_py + c, rr * n_py + cc))
        blocks[8 - q] = lax.ppermute(parcel[q], AXES, pairs)
    blocks[4] = jnp.zeros_like(parcel[4])
    return jnp.concatenate(blocks, axis=0)


def butterfly_sum(value):
    for axis in ("py", "px"):
        size = lax.axis_size(axis)
        step = 1
        while step < size:
            pairs = [(i, i ^ step) for i in range(size)]
            value = value + lax.ppermute(value, axis, pairs)
            step *= 2
    return value


def local(
    prim_elem,
    forcing,
    adj_source,
    elem_volume,
    face_link,
    send_map,
    elem_count,
    prolong_elem,
    face_trace,
    prolong_face,
    stiffness,
    conv_grad,
    conv_out,
    lift,
    adj_trace,
    adj_lift,
    block_corr,
):
    elems = face_link.shape[1]
    face_total = 4 * elems
    slot_total = send_map.shape[1]
    src_total = face_total + slot_total
    slot_row = jnp.clip(send_map[0], 0, face_total)
    link = jnp.clip(face_link.reshape(-1), 0, src_total)
    width = prolong_face.shape[0]

    coarse = jnp.einsum(
        "jrc,ce->jer", face_trace, prim_elem, preferred_element_type=jnp.float32
    ).astype(jnp.bfloat16)
    own_trace = jnp.einsum("jer,fr->jef", coarse, prolong_face, preferred_element_type=jnp.float32)
    own_rows = own_trace.reshape(face_total, -1)

    source = adj_source.astype(jnp.float32)
    adjoint = source + jnp.dot(block_corr, adj_source, preferred_element_type=jnp.float32)

    def adj_faces(adjoint):
        face_vals = jnp.einsum(
            "jrv,ve->jer",
            adj_trace,
            adjoint.astype(jnp.bfloat16),
            preferred_element_type=jnp.float32,
        ).astype(jnp.bfloat16)
        return face_vals.reshape(face_total, -1)

    def sweep_tail(partner, adjoint_unused=None):
        coupling = jnp.einsum(
            "vjr,jer->ve", adj_lift, partner.reshape(4, elems, -1), preferred_element_type=jnp.float32
        )
        right_side = source - coupling
        return right_side + jnp.dot(
            block_corr, right_side.astype(jnp.bfloat16), preferred_element_type=jnp.float32
        )

    zero_row = lambda w: jnp.zeros((1, w), jnp.float32)

    face_rows = adj_faces(adjoint)
    both = jnp.concatenate([own_rows, face_rows.astype(jnp.float32)], axis=1)
    both_pad = jnp.concatenate([both, zero_row(2 * width)], axis=0)
    parcel = take_rows(both_pad, slot_row).astype(jnp.bfloat16)
    received = exchange(parcel.reshape(9, -1, 2 * width)).astype(jnp.float32)
    pool = jnp.concatenate([both, received, zero_row(2 * width)], axis=0)
    picked = take_rows(pool, link)
    neighbour = picked[:, :width]
    partner = picked[:, width:].astype(jnp.bfloat16)
    adjoint = sweep_tail(partner)

    for sweep_index in range(1, SWEEPS):
        face_rows = adj_faces(adjoint).astype(jnp.float32)
        face_pad = jnp.concatenate([face_rows, zero_row(width)], axis=0)
        parcel = take_rows(face_pad, slot_row).astype(jnp.bfloat16)
        received = exchange(parcel.reshape(9, -1, width)).astype(jnp.float32)
        pool = jnp.concatenate([face_rows, received, zero_row(width)], axis=0)
        partner = take_rows(pool, link).astype(jnp.bfloat16)
        adjoint = sweep_tail(partner)

    state_elem = jnp.dot(prolong_elem, prim_elem, preferred_element_type=jnp.float32).astype(
        jnp.bfloat16
    )
    conv_in = jnp.dot(conv_grad, state_elem, preferred_element_type=jnp.float32)
    conv_flux = (state_elem * conv_in).astype(jnp.bfloat16)
    trace_jump = (own_rows - neighbour).astype(jnp.bfloat16).reshape(4, elems, -1)
    residual = jnp.dot(stiffness, state_elem, preferred_element_type=jnp.float32)
    residual = residual + jnp.dot(conv_out, conv_flux, preferred_element_type=jnp.float32)
    residual = (
        residual
        + jnp.einsum("vjr,jer->ve", lift, trace_jump, preferred_element_type=jnp.float32)
        - forcing.astype(jnp.float32)
    )
    measure = jnp.abs(jnp.sum(adjoint * residual, axis=0))
    alive = jnp.arange(measure.shape[0]) < elem_count[0]
    weighted = jnp.where(alive, elem_volume * measure, 0.0)
    totals = butterfly_sum(
        jnp.stack([jnp.sum(weighted), elem_count[0].astype(jnp.float32)])
    )
    mean_error = totals[0] / totals[1]
    return (weighted / mean_error, jnp.reshape(mean_error, (1,)))


def solution(mesh):
    placed = (
        P(None, AXES),
        P(None, AXES),
        P(None, AXES),
        P(AXES),
        P(None, AXES),
        P(AXES, None),
        P(AXES),
        P(),
        P(),
        P(),
        P(),
        P(),
        P(),
        P(),
        P(),
        P(),
        P(),
    )
    return jax.shard_map(
        local, mesh=mesh, in_specs=placed, out_specs=(P(AXES), P()), check_vma=False
    )
```

```python
import jax
import jax.numpy as jnp
from jax import lax
from jax.experimental import pallas as pl
from jax.experimental.pallas import tpu as pltpu
from jax.sharding import PartitionSpec as P

SWEEPS = 2
AXES = ("px", "py")


def _send_kernel(idx_ref, own_ref, out_ref):
    faces = own_ref.shape[0]

    def body(i, carry):
        row = idx_ref[i]
        value = own_ref[pl.ds(jnp.minimum(row, faces - 1), 1), :]
        out_ref[pl.ds(i, 1), :] = jnp.where(row < faces, value, 0.0)
        return carry

    lax.fori_loop(0, out_ref.shape[0], body, 0, unroll=16)


def _pull_kernel(idx_ref, own_ref, *refs):
    blocks, out_ref, pool = refs[:8], refs[8], refs[9]
    faces, width = own_ref.shape
    slots = blocks[0].shape[0]
    chunk = 256

    def copy_own(i, carry):
        at = pl.multiple_of(i * chunk, chunk)
        pool[pl.ds(at, chunk), :] = own_ref[pl.ds(at, chunk), :]
        return carry

    lax.fori_loop(0, faces // chunk, copy_own, 0)
    for slot, block in zip((0, 1, 2, 3, 5, 6, 7, 8), blocks):
        pool[pl.ds(faces + slot * slots, slots), :] = block[...].astype(jnp.float32)
    pool[pl.ds(faces + 4 * slots, slots), :] = jnp.zeros((slots, width), jnp.float32)
    pool[pl.ds(faces + 9 * slots, 8), :] = jnp.zeros((8, width), jnp.float32)

    def body(i, carry):
        row = idx_ref[i]
        out_ref[pl.ds(i, 1), :] = pool[pl.ds(row, 1), :]
        return carry

    lax.fori_loop(0, out_ref.shape[0], body, 0, unroll=16)


_VMEM = dict(compiler_params=pltpu.CompilerParams(vmem_limit_bytes=48 * 1024 * 1024))


def send_rows(own, index):
    count, width = index.shape[0], own.shape[1]
    return pl.pallas_call(
        _send_kernel,
        out_shape=jax.ShapeDtypeStruct((count, width), own.dtype),
        in_specs=[
            pl.BlockSpec(memory_space=pltpu.SMEM),
            pl.BlockSpec(memory_space=pltpu.VMEM),
        ],
        out_specs=pl.BlockSpec(memory_space=pltpu.VMEM),
        cost_estimate=pl.CostEstimate(
            flops=0, transcendentals=0, bytes_accessed=2 * count * width * 4
        ),
        **_VMEM,
    )(index, own)


def pull_rows(own, blocks, index):
    count, width = index.shape[0], own.shape[1]
    faces, slots = own.shape[0], blocks[0].shape[0]
    return pl.pallas_call(
        _pull_kernel,
        out_shape=jax.ShapeDtypeStruct((count, width), own.dtype),
        in_specs=[pl.BlockSpec(memory_space=pltpu.SMEM)]
        + [pl.BlockSpec(memory_space=pltpu.VMEM)] * (1 + len(blocks)),
        out_specs=pl.BlockSpec(memory_space=pltpu.VMEM),
        scratch_shapes=[pltpu.VMEM((faces + 9 * slots + 8, width), jnp.float32)],
        cost_estimate=pl.CostEstimate(
            flops=0, transcendentals=0, bytes_accessed=3 * count * width * 4
        ),
        **_VMEM,
    )(index, own, *blocks)


def exchange(parcel):
    n_px = lax.axis_size("px")
    n_py = lax.axis_size("py")
    blocks = [None] * 9
    for q in range(9):
        if q == 4:
            continue
        da, db = q // 3 - 1, q % 3 - 1
        pairs = []
        for r in range(n_px):
            for c in range(n_py):
                rr, cc = r + da, c + db
                if 0 <= rr < n_px and 0 <= cc < n_py:
                    pairs.append((r * n_py + c, rr * n_py + cc))
        blocks[8 - q] = lax.ppermute(parcel[q], AXES, pairs)
    return [blocks[t] for t in (0, 1, 2, 3, 5, 6, 7, 8)]


def butterfly_sum(value):
    for axis in ("py", "px"):
        size = lax.axis_size(axis)
        step = 1
        while step < size:
            pairs = [(i, i ^ step) for i in range(size)]
            value = value + lax.ppermute(value, axis, pairs)
            step *= 2
    return value


def local(
    prim_elem,
    forcing,
    adj_source,
    elem_volume,
    face_link,
    send_map,
    elem_count,
    prolong_elem,
    face_trace,
    prolong_face,
    stiffness,
    conv_grad,
    conv_out,
    lift,
    adj_trace,
    adj_lift,
    block_corr,
):
    elems = face_link.shape[1]
    face_total = 4 * elems
    slot_total = send_map.shape[1]
    src_total = face_total + slot_total
    slot_row = jnp.clip(send_map[0], 0, face_total)
    link = jnp.clip(face_link.reshape(-1), 0, src_total)
    width = prolong_face.shape[0]

    lanes, half = 128, 64
    bf = jnp.bfloat16
    face_w = jnp.zeros((lanes, prolong_face.shape[1]), bf).at[:width].set(prolong_face)
    trace_w = jnp.zeros((4, lanes, adj_trace.shape[2]), bf).at[:, half : half + width].set(adj_trace)
    couple_w = jnp.zeros((adj_lift.shape[0], 4, lanes), bf).at[:, :, half : half + width].set(adj_lift)
    lift_w = jnp.zeros((lift.shape[0], 4, lanes), bf).at[:, :, :width].set(lift)

    coarse = jnp.einsum(
        "jrc,ce->jer", face_trace, prim_elem, preferred_element_type=jnp.float32
    ).astype(bf)
    own_rows = jnp.einsum(
        "jer,fr->jef", coarse, face_w, preferred_element_type=jnp.float32
    ).reshape(face_total, lanes)

    source = adj_source.astype(jnp.float32)
    adjoint = source + jnp.dot(block_corr, adj_source, preferred_element_type=jnp.float32)

    def adj_faces(adjoint):
        face_vals = jnp.einsum(
            "jrv,ve->jer", trace_w, adjoint.astype(bf), preferred_element_type=jnp.float32
        ).astype(bf)
        return face_vals.astype(jnp.float32).reshape(face_total, lanes)

    def sweep(rows):
        parcel = send_rows(rows, slot_row).astype(bf)
        blocks = exchange(parcel.reshape(9, -1, lanes))
        picked = pull_rows(rows, blocks, link)
        coupling = jnp.einsum(
            "vjr,jer->ve",
            couple_w,
            picked.astype(bf).reshape(4, elems, lanes),
            preferred_element_type=jnp.float32,
        )
        right_side = source - coupling
        adjoint = right_side + jnp.dot(
            block_corr, right_side.astype(bf), preferred_element_type=jnp.float32
        )
        return picked, adjoint

    picked, adjoint = sweep(own_rows + adj_faces(adjoint))
    for sweep_index in range(1, SWEEPS):
        _, adjoint = sweep(adj_faces(adjoint))

    state_elem = jnp.dot(prolong_elem, prim_elem, preferred_element_type=jnp.float32).astype(
        jnp.bfloat16
    )
    conv_in = jnp.dot(conv_grad, state_elem, preferred_element_type=jnp.float32)
    conv_flux = (state_elem * conv_in).astype(jnp.bfloat16)
    trace_jump = (own_rows - picked).astype(bf).reshape(4, elems, lanes)
    residual = jnp.dot(stiffness, state_elem, preferred_element_type=jnp.float32)
    residual = residual + jnp.dot(conv_out, conv_flux, preferred_element_type=jnp.float32)
    residual = (
        residual
        + jnp.einsum("vjr,jer->ve", lift_w, trace_jump, preferred_element_type=jnp.float32)
        - forcing.astype(jnp.float32)
    )
    measure = jnp.abs(jnp.sum(adjoint * residual, axis=0))
    alive = jnp.arange(measure.shape[0]) < elem_count[0]
    weighted = jnp.where(alive, elem_volume * measure, 0.0)
    totals = butterfly_sum(
        jnp.stack([jnp.sum(weighted), elem_count[0].astype(jnp.float32)])
    )
    mean_error = totals[0] / totals[1]
    return (weighted / mean_error, jnp.reshape(mean_error, (1,)))


def solution(mesh):
    placed = (
        P(None, AXES),
        P(None, AXES),
        P(None, AXES),
        P(AXES),
        P(None, AXES),
        P(AXES, None),
        P(AXES),
        P(),
        P(),
        P(),
        P(),
        P(),
        P(),
        P(),
        P(),
        P(),
        P(),
    )
    return jax.shard_map(
        local, mesh=mesh, in_specs=placed, out_specs=(P(AXES), P()), check_vma=False
    )
```

```python
import jax
import jax.numpy as jnp
from jax import lax
from jax.experimental import pallas as pl
from jax.experimental.pallas import tpu as pltpu
from jax.sharding import PartitionSpec as P

SWEEPS = 2
AXES = ("px", "py")


def _send_kernel(idx_ref, own_ref, out_ref):
    faces = own_ref.shape[0]

    def body(i, carry):
        row = idx_ref[i]
        value = own_ref[pl.ds(jnp.minimum(row, faces - 1), 1), :]
        out_ref[pl.ds(i, 1), :] = jnp.where(row < faces, value, 0.0)
        return carry

    lax.fori_loop(0, out_ref.shape[0], body, 0, unroll=16)


def _pull_kernel(idx_ref, own_ref, *refs):
    blocks, out_ref, pool = refs[:8], refs[8], refs[9]
    faces, width = own_ref.shape
    slots = blocks[0].shape[0]
    chunk = 256

    def copy_own(i, carry):
        at = pl.multiple_of(i * chunk, chunk)
        pool[pl.ds(at, chunk), :] = own_ref[pl.ds(at, chunk), :]
        return carry

    lax.fori_loop(0, faces // chunk, copy_own, 0)
    for slot, block in zip((0, 1, 2, 3, 5, 6, 7, 8), blocks):
        pool[pl.ds(faces + slot * slots, slots), :] = block[...].astype(jnp.float32)
    pool[pl.ds(faces + 4 * slots, slots), :] = jnp.zeros((slots, width), jnp.float32)
    pool[pl.ds(faces + 9 * slots, 8), :] = jnp.zeros((8, width), jnp.float32)

    def body(i, carry):
        row = idx_ref[i]
        out_ref[pl.ds(i, 1), :] = pool[pl.ds(row, 1), :]
        return carry

    lax.fori_loop(0, out_ref.shape[0], body, 0, unroll=16)


_VMEM = dict(compiler_params=pltpu.CompilerParams(vmem_limit_bytes=48 * 1024 * 1024))


def send_rows(own, index):
    count, width = index.shape[0], own.shape[1]
    return pl.pallas_call(
        _send_kernel,
        out_shape=jax.ShapeDtypeStruct((count, width), own.dtype),
        in_specs=[
            pl.BlockSpec(memory_space=pltpu.SMEM),
            pl.BlockSpec(memory_space=pltpu.VMEM),
        ],
        out_specs=pl.BlockSpec(memory_space=pltpu.VMEM),
        cost_estimate=pl.CostEstimate(
            flops=0, transcendentals=0, bytes_accessed=2 * count * width * 4
        ),
        **_VMEM,
    )(index, own)


def pull_rows(own, blocks, index):
    count, width = index.shape[0], own.shape[1]
    faces, slots = own.shape[0], blocks[0].shape[0]
    return pl.pallas_call(
        _pull_kernel,
        out_shape=jax.ShapeDtypeStruct((count, width), own.dtype),
        in_specs=[pl.BlockSpec(memory_space=pltpu.SMEM)]
        + [pl.BlockSpec(memory_space=pltpu.VMEM)] * (1 + len(blocks)),
        out_specs=pl.BlockSpec(memory_space=pltpu.VMEM),
        scratch_shapes=[pltpu.VMEM((faces + 9 * slots + 8, width), jnp.float32)],
        cost_estimate=pl.CostEstimate(
            flops=0, transcendentals=0, bytes_accessed=3 * count * width * 4
        ),
        **_VMEM,
    )(index, own, *blocks)


def exchange(parcel):
    n_px = lax.axis_size("px")
    n_py = lax.axis_size("py")
    blocks = [None] * 9
    for q in range(9):
        if q == 4:
            continue
        da, db = q // 3 - 1, q % 3 - 1
        pairs = []
        for r in range(n_px):
            for c in range(n_py):
                rr, cc = r + da, c + db
                if 0 <= rr < n_px and 0 <= cc < n_py:
                    pairs.append((r * n_py + c, rr * n_py + cc))
        blocks[8 - q] = lax.ppermute(parcel[q], AXES, pairs)
    return [blocks[t] for t in (0, 1, 2, 3, 5, 6, 7, 8)]


def butterfly_sum(value):
    n_py = lax.axis_size("py")
    total = lax.axis_size("px") * n_py
    bits = total.bit_length() - 1
    masks = [1 << b for b in range(bits)]
    for a, b in zip(masks[0::2], masks[1::2]):
        got = {}
        for m in (a, b, a ^ b):
            got[m] = lax.ppermute(value, AXES, [(i, i ^ m) for i in range(total)])
        value = (value + got[a]) + (got[b] + got[a ^ b])
    return value


def local(
    prim_elem,
    forcing,
    adj_source,
    elem_volume,
    face_link,
    send_map,
    elem_count,
    prolong_elem,
    face_trace,
    prolong_face,
    stiffness,
    conv_grad,
    conv_out,
    lift,
    adj_trace,
    adj_lift,
    block_corr,
):
    elems = face_link.shape[1]
    face_total = 4 * elems
    slot_total = send_map.shape[1]
    src_total = face_total + slot_total
    slot_row = jnp.clip(send_map[0], 0, face_total)
    link = jnp.clip(face_link.reshape(-1), 0, src_total)
    width = prolong_face.shape[0]

    lanes, half = 128, 64
    bf = jnp.bfloat16
    face_w = jnp.zeros((lanes, prolong_face.shape[1]), bf).at[:width].set(prolong_face)
    trace_w = jnp.zeros((4, lanes, adj_trace.shape[2]), bf).at[:, half : half + width].set(adj_trace)
    couple_w = jnp.zeros((adj_lift.shape[0], 4, lanes), bf).at[:, :, half : half + width].set(adj_lift)
    lift_w = jnp.zeros((lift.shape[0], 4, lanes), bf).at[:, :, :width].set(lift)

    coarse = jnp.einsum(
        "jrc,ce->jer", face_trace, prim_elem, preferred_element_type=jnp.float32
    ).astype(bf)
    own_rows = jnp.einsum(
        "jer,fr->jef", coarse, face_w, preferred_element_type=jnp.float32
    ).reshape(face_total, lanes)

    source = adj_source.astype(jnp.float32)
    adjoint = source + jnp.dot(block_corr, adj_source, preferred_element_type=jnp.float32)

    def adj_faces(adjoint):
        face_vals = jnp.einsum(
            "jrv,ve->jer", trace_w, adjoint.astype(bf), preferred_element_type=jnp.float32
        ).astype(bf)
        return face_vals.astype(jnp.float32).reshape(face_total, lanes)

    def sweep(rows):
        parcel = send_rows(rows, slot_row).astype(bf)
        blocks = exchange(parcel.reshape(9, -1, lanes))
        picked = pull_rows(rows, blocks, link)
        coupling = jnp.einsum(
            "vjr,jer->ve",
            couple_w,
            picked.astype(bf).reshape(4, elems, lanes),
            preferred_element_type=jnp.float32,
        )
        right_side = source - coupling
        adjoint = right_side + jnp.dot(
            block_corr, right_side.astype(bf), preferred_element_type=jnp.float32
        )
        return picked, adjoint

    picked, adjoint = sweep(own_rows + adj_faces(adjoint))
    for sweep_index in range(1, SWEEPS):
        _, adjoint = sweep(adj_faces(adjoint))

    state_elem = jnp.dot(prolong_elem, prim_elem, preferred_element_type=jnp.float32).astype(
        jnp.bfloat16
    )
    conv_in = jnp.dot(conv_grad, state_elem, preferred_element_type=jnp.float32)
    conv_flux = (state_elem * conv_in).astype(jnp.bfloat16)
    trace_jump = (own_rows - picked).astype(bf).reshape(4, elems, lanes)
    residual = jnp.dot(stiffness, state_elem, preferred_element_type=jnp.float32)
    residual = residual + jnp.dot(conv_out, conv_flux, preferred_element_type=jnp.float32)
    residual = (
        residual
        + jnp.einsum("vjr,jer->ve", lift_w, trace_jump, preferred_element_type=jnp.float32)
        - forcing.astype(jnp.float32)
    )
    measure = jnp.abs(jnp.sum(adjoint * residual, axis=0))
    alive = jnp.arange(measure.shape[0]) < elem_count[0]
    weighted = jnp.where(alive, elem_volume * measure, 0.0)
    totals = butterfly_sum(
        jnp.stack([jnp.sum(weighted), elem_count[0].astype(jnp.float32)])
    )
    mean_error = totals[0] / totals[1]
    return (weighted / mean_error, jnp.reshape(mean_error, (1,)))


def solution(mesh):
    placed = (
        P(None, AXES),
        P(None, AXES),
        P(None, AXES),
        P(AXES),
        P(None, AXES),
        P(AXES, None),
        P(AXES),
        P(),
        P(),
        P(),
        P(),
        P(),
        P(),
        P(),
        P(),
        P(),
        P(),
    )
    return jax.shard_map(
        local, mesh=mesh, in_specs=placed, out_specs=(P(AXES), P()), check_vma=False
    )
```

```python
import jax
import jax.numpy as jnp
from jax import lax
from jax.experimental import pallas as pl
from jax.experimental.pallas import tpu as pltpu
from jax.sharding import PartitionSpec as P

SWEEPS = 2
AXES = ("px", "py")


def _send_kernel(idx_ref, own_ref, out_ref, pool):
    faces, width = own_ref.shape
    chunk = 256

    def copy_own(i, carry):
        at = pl.multiple_of(i * chunk, chunk)
        pool[pl.ds(at, chunk), :] = own_ref[pl.ds(at, chunk), :]
        return carry

    lax.fori_loop(0, faces // chunk, copy_own, 0)
    pool[pl.ds(faces, 8), :] = jnp.zeros((8, width), jnp.float32)

    def body(i, carry):
        row = idx_ref[i]
        out_ref[pl.ds(i, 1), :] = pool[pl.ds(row, 1), :]
        return carry

    lax.fori_loop(0, out_ref.shape[0], body, 0, unroll=16)


def _pull_kernel(idx_ref, own_ref, *refs):
    blocks, out_ref, pool = refs[:8], refs[8], refs[9]
    faces, width = own_ref.shape
    slots = blocks[0].shape[0]
    chunk = 256

    def copy_own(i, carry):
        at = pl.multiple_of(i * chunk, chunk)
        pool[pl.ds(at, chunk), :] = own_ref[pl.ds(at, chunk), :]
        return carry

    lax.fori_loop(0, faces // chunk, copy_own, 0)
    for slot, block in zip((0, 1, 2, 3, 5, 6, 7, 8), blocks):
        pool[pl.ds(faces + slot * slots, slots), :] = block[...].astype(jnp.float32)
    pool[pl.ds(faces + 4 * slots, slots), :] = jnp.zeros((slots, width), jnp.float32)
    pool[pl.ds(faces + 9 * slots, 8), :] = jnp.zeros((8, width), jnp.float32)

    def body(i, carry):
        row = idx_ref[i]
        out_ref[pl.ds(i, 1), :] = pool[pl.ds(row, 1), :]
        return carry

    lax.fori_loop(0, out_ref.shape[0], body, 0, unroll=16)


_VMEM = dict(compiler_params=pltpu.CompilerParams(vmem_limit_bytes=48 * 1024 * 1024))


def send_rows(own, index):
    count, width = index.shape[0], own.shape[1]
    return pl.pallas_call(
        _send_kernel,
        out_shape=jax.ShapeDtypeStruct((count, width), own.dtype),
        in_specs=[
            pl.BlockSpec(memory_space=pltpu.SMEM),
            pl.BlockSpec(memory_space=pltpu.VMEM),
        ],
        out_specs=pl.BlockSpec(memory_space=pltpu.VMEM),
        scratch_shapes=[pltpu.VMEM((own.shape[0] + 8, width), jnp.float32)],
        cost_estimate=pl.CostEstimate(
            flops=0, transcendentals=0, bytes_accessed=2 * count * width * 4
        ),
        **_VMEM,
    )(index, own)


def pull_rows(own, blocks, index):
    count, width = index.shape[0], own.shape[1]
    faces, slots = own.shape[0], blocks[0].shape[0]
    return pl.pallas_call(
        _pull_kernel,
        out_shape=jax.ShapeDtypeStruct((count, width), own.dtype),
        in_specs=[pl.BlockSpec(memory_space=pltpu.SMEM)]
        + [pl.BlockSpec(memory_space=pltpu.VMEM)] * (1 + len(blocks)),
        out_specs=pl.BlockSpec(memory_space=pltpu.VMEM),
        scratch_shapes=[pltpu.VMEM((faces + 9 * slots + 8, width), jnp.float32)],
        cost_estimate=pl.CostEstimate(
            flops=0, transcendentals=0, bytes_accessed=3 * count * width * 4
        ),
        **_VMEM,
    )(index, own, *blocks)


def exchange(parcel):
    n_px = lax.axis_size("px")
    n_py = lax.axis_size("py")
    blocks = [None] * 9
    for q in range(9):
        if q == 4:
            continue
        da, db = q // 3 - 1, q % 3 - 1
        pairs = []
        for r in range(n_px):
            for c in range(n_py):
                rr, cc = r + da, c + db
                if 0 <= rr < n_px and 0 <= cc < n_py:
                    pairs.append((r * n_py + c, rr * n_py + cc))
        blocks[8 - q] = lax.ppermute(parcel[q], AXES, pairs)
    return [blocks[t] for t in (0, 1, 2, 3, 5, 6, 7, 8)]


def butterfly_sum(value):
    n_py = lax.axis_size("py")
    total = lax.axis_size("px") * n_py
    bits = total.bit_length() - 1
    masks = [1 << b for b in range(bits)]
    for a, b in zip(masks[0::2], masks[1::2]):
        got = {}
        for m in (a, b, a ^ b):
            got[m] = lax.ppermute(value, AXES, [(i, i ^ m) for i in range(total)])
        value = (value + got[a]) + (got[b] + got[a ^ b])
    return value


def local(
    prim_elem,
    forcing,
    adj_source,
    elem_volume,
    face_link,
    send_map,
    elem_count,
    prolong_elem,
    face_trace,
    prolong_face,
    stiffness,
    conv_grad,
    conv_out,
    lift,
    adj_trace,
    adj_lift,
    block_corr,
):
    elems = face_link.shape[1]
    face_total = 4 * elems
    slot_total = send_map.shape[1]
    src_total = face_total + slot_total
    slot_row = jnp.clip(send_map[0], 0, face_total)
    link = jnp.clip(face_link.reshape(-1), 0, src_total)
    width = prolong_face.shape[0]

    lanes, half = 128, 64
    bf = jnp.bfloat16
    face_w = jnp.zeros((lanes, prolong_face.shape[1]), bf).at[:width].set(prolong_face)
    trace_w = jnp.zeros((4, lanes, adj_trace.shape[2]), bf).at[:, half : half + width].set(adj_trace)
    couple_w = jnp.zeros((adj_lift.shape[0], 4, lanes), bf).at[:, :, half : half + width].set(adj_lift)
    lift_w = jnp.zeros((lift.shape[0], 4, lanes), bf).at[:, :, :width].set(lift)

    coarse = jnp.einsum(
        "jrc,ce->jer", face_trace, prim_elem, preferred_element_type=jnp.float32
    ).astype(bf)
    own_rows = jnp.einsum(
        "jer,fr->jef", coarse, face_w, preferred_element_type=jnp.float32
    ).reshape(face_total, lanes)

    source = adj_source.astype(jnp.float32)
    adjoint = source + jnp.dot(block_corr, adj_source, preferred_element_type=jnp.float32)

    def adj_faces(adjoint):
        face_vals = jnp.einsum(
            "jrv,ve->jer", trace_w, adjoint.astype(bf), preferred_element_type=jnp.float32
        ).astype(bf)
        return face_vals.astype(jnp.float32).reshape(face_total, lanes)

    def sweep(rows):
        parcel = send_rows(rows, slot_row).astype(bf)
        blocks = exchange(parcel.reshape(9, -1, lanes))
        picked = pull_rows(rows, blocks, link)
        coupling = jnp.einsum(
            "vjr,jer->ve",
            couple_w,
            picked.astype(bf).reshape(4, elems, lanes),
            preferred_element_type=jnp.float32,
        )
        right_side = source - coupling
        adjoint = right_side + jnp.dot(
            block_corr, right_side.astype(bf), preferred_element_type=jnp.float32
        )
        return picked, adjoint

    picked, adjoint = sweep(own_rows + adj_faces(adjoint))
    for sweep_index in range(1, SWEEPS):
        _, adjoint = sweep(adj_faces(adjoint))

    state_elem = jnp.dot(prolong_elem, prim_elem, preferred_element_type=jnp.float32).astype(
        jnp.bfloat16
    )
    conv_in = jnp.dot(conv_grad, state_elem, preferred_element_type=jnp.float32)
    conv_flux = (state_elem * conv_in).astype(jnp.bfloat16)
    trace_jump = (own_rows - picked).astype(bf).reshape(4, elems, lanes)
    residual = jnp.dot(stiffness, state_elem, preferred_element_type=jnp.float32)
    residual = residual + jnp.dot(conv_out, conv_flux, preferred_element_type=jnp.float32)
    residual = (
        residual
        + jnp.einsum("vjr,jer->ve", lift_w, trace_jump, preferred_element_type=jnp.float32)
        - forcing.astype(jnp.float32)
    )
    measure = jnp.abs(jnp.sum(adjoint * residual, axis=0))
    alive = jnp.arange(measure.shape[0]) < elem_count[0]
    weighted = jnp.where(alive, elem_volume * measure, 0.0)
    totals = butterfly_sum(
        jnp.stack([jnp.sum(weighted), elem_count[0].astype(jnp.float32)])
    )
    mean_error = totals[0] / totals[1]
    return (weighted / mean_error, jnp.reshape(mean_error, (1,)))


def solution(mesh):
    placed = (
        P(None, AXES),
        P(None, AXES),
        P(None, AXES),
        P(AXES),
        P(None, AXES),
        P(AXES, None),
        P(AXES),
        P(),
        P(),
        P(),
        P(),
        P(),
        P(),
        P(),
        P(),
        P(),
        P(),
    )
    return jax.shard_map(
        local, mesh=mesh, in_specs=placed, out_specs=(P(AXES), P()), check_vma=False
    )
```

```python
import functools

import jax
import jax.numpy as jnp
from jax import lax
from jax.experimental import pallas as pl
from jax.experimental.pallas import tpu as pltpu
from jax.sharding import PartitionSpec as P

SWEEPS = 2
AXES = ("px", "py")


def _fill_pool(pool, parts):
    faces = parts[0].shape[0]
    chunk = 256

    def copy_own(i, carry):
        at = pl.multiple_of(i * chunk, chunk)
        total = parts[0][pl.ds(at, chunk), :].astype(jnp.float32)
        for part in parts[1:]:
            total = total + part[pl.ds(at, chunk), :].astype(jnp.float32)
        pool[pl.ds(at, chunk), :] = total
        return carry

    lax.fori_loop(0, faces // chunk, copy_own, 0)


def _gather_loop(idx_ref, pool, out_ref):
    def body(i, carry):
        row = idx_ref[i]
        out_ref[pl.ds(i, 1), :] = pool[pl.ds(row, 1), :]
        return carry

    lax.fori_loop(0, out_ref.shape[0], body, 0, unroll=16)


def _send_kernel(n_parts, idx_ref, *refs):
    parts, out_ref, pool = refs[:n_parts], refs[n_parts], refs[n_parts + 1]
    faces, width = parts[0].shape
    _fill_pool(pool, parts)
    pool[pl.ds(faces, 8), :] = jnp.zeros((8, width), jnp.float32)
    _gather_loop(idx_ref, pool, out_ref)


def _pull_kernel(n_parts, idx_ref, *refs):
    parts = refs[:n_parts]
    blocks = refs[n_parts : n_parts + 8]
    out_ref, pool = refs[n_parts + 8], refs[n_parts + 9]
    faces, width = parts[0].shape
    slots = blocks[0].shape[0]
    _fill_pool(pool, parts)
    for slot, block in zip((0, 1, 2, 3, 5, 6, 7, 8), blocks):
        pool[pl.ds(faces + slot * slots, slots), :] = block[...].astype(jnp.float32)
    pool[pl.ds(faces + 4 * slots, slots), :] = jnp.zeros((slots, width), jnp.float32)
    pool[pl.ds(faces + 9 * slots, 8), :] = jnp.zeros((8, width), jnp.float32)
    _gather_loop(idx_ref, pool, out_ref)


_VMEM = dict(compiler_params=pltpu.CompilerParams(vmem_limit_bytes=48 * 1024 * 1024))


def send_rows(parts, index):
    count, (faces, width) = index.shape[0], parts[0].shape
    return pl.pallas_call(
        functools.partial(_send_kernel, len(parts)),
        out_shape=jax.ShapeDtypeStruct((count, width), jnp.float32),
        in_specs=[pl.BlockSpec(memory_space=pltpu.SMEM)]
        + [pl.BlockSpec(memory_space=pltpu.VMEM)] * len(parts),
        out_specs=pl.BlockSpec(memory_space=pltpu.VMEM),
        scratch_shapes=[pltpu.VMEM((faces + 8, width), jnp.float32)],
        cost_estimate=pl.CostEstimate(
            flops=0, transcendentals=0, bytes_accessed=2 * count * width * 4
        ),
        **_VMEM,
    )(index, *parts)


def pull_rows(parts, blocks, index):
    count, (faces, width) = index.shape[0], parts[0].shape
    slots = blocks[0].shape[0]
    return pl.pallas_call(
        functools.partial(_pull_kernel, len(parts)),
        out_shape=jax.ShapeDtypeStruct((count, width), jnp.float32),
        in_specs=[pl.BlockSpec(memory_space=pltpu.SMEM)]
        + [pl.BlockSpec(memory_space=pltpu.VMEM)] * (len(parts) + len(blocks)),
        out_specs=pl.BlockSpec(memory_space=pltpu.VMEM),
        scratch_shapes=[pltpu.VMEM((faces + 9 * slots + 8, width), jnp.float32)],
        cost_estimate=pl.CostEstimate(
            flops=0, transcendentals=0, bytes_accessed=3 * count * width * 4
        ),
        **_VMEM,
    )(index, *parts, *blocks)


def exchange(parcel):
    n_px = lax.axis_size("px")
    n_py = lax.axis_size("py")
    blocks = [None] * 9
    for q in range(9):
        if q == 4:
            continue
        da, db = q // 3 - 1, q % 3 - 1
        pairs = []
        for r in range(n_px):
            for c in range(n_py):
                rr, cc = r + da, c + db
                if 0 <= rr < n_px and 0 <= cc < n_py:
                    pairs.append((r * n_py + c, rr * n_py + cc))
        blocks[8 - q] = lax.ppermute(parcel[q], AXES, pairs)
    return [blocks[t] for t in (0, 1, 2, 3, 5, 6, 7, 8)]


def butterfly_sum(value):
    n_py = lax.axis_size("py")
    total = lax.axis_size("px") * n_py
    bits = total.bit_length() - 1
    masks = [1 << b for b in range(bits)]
    for a, b in zip(masks[0::2], masks[1::2]):
        got = {}
        for m in (a, b, a ^ b):
            got[m] = lax.ppermute(value, AXES, [(i, i ^ m) for i in range(total)])
        value = (value + got[a]) + (got[b] + got[a ^ b])
    return value


def local(
    prim_elem,
    forcing,
    adj_source,
    elem_volume,
    face_link,
    send_map,
    elem_count,
    prolong_elem,
    face_trace,
    prolong_face,
    stiffness,
    conv_grad,
    conv_out,
    lift,
    adj_trace,
    adj_lift,
    block_corr,
):
    elems = face_link.shape[1]
    face_total = 4 * elems
    slot_total = send_map.shape[1]
    src_total = face_total + slot_total
    slot_row = jnp.clip(send_map[0], 0, face_total)
    link = jnp.clip(face_link.reshape(-1), 0, src_total)
    width = prolong_face.shape[0]

    lanes, half = 128, 64
    bf = jnp.bfloat16
    face_w = jnp.zeros((lanes, prolong_face.shape[1]), bf).at[:width].set(prolong_face)
    trace_w = jnp.zeros((4, lanes, adj_trace.shape[2]), bf).at[:, half : half + width].set(adj_trace)
    couple_w = jnp.zeros((adj_lift.shape[0], 4, lanes), bf).at[:, :, half : half + width].set(adj_lift)
    lift_w = jnp.zeros((lift.shape[0], 4, lanes), bf).at[:, :, :width].set(lift)

    coarse = jnp.einsum(
        "jrc,ce->jer", face_trace, prim_elem, preferred_element_type=jnp.float32
    ).astype(bf)
    own_rows = jnp.einsum(
        "jer,fr->jef", coarse, face_w, preferred_element_type=jnp.float32
    ).reshape(face_total, lanes)

    source = adj_source.astype(jnp.float32)
    adjoint = source + jnp.dot(block_corr, adj_source, preferred_element_type=jnp.float32)

    def adj_faces(adjoint):
        face_vals = jnp.einsum(
            "jrv,ve->jer", trace_w, adjoint.astype(bf), preferred_element_type=jnp.float32
        ).astype(bf)
        return face_vals.reshape(face_total, lanes)

    def sweep(parts):
        parcel = send_rows(parts, slot_row).astype(bf)
        blocks = exchange(parcel.reshape(9, -1, lanes))
        picked = pull_rows(parts, blocks, link)
        coupling = jnp.einsum(
            "vjr,jer->ve",
            couple_w,
            picked.astype(bf).reshape(4, elems, lanes),
            preferred_element_type=jnp.float32,
        )
        right_side = source - coupling
        adjoint = right_side + jnp.dot(
            block_corr, right_side.astype(bf), preferred_element_type=jnp.float32
        )
        return picked, adjoint

    picked, adjoint = sweep([own_rows, adj_faces(adjoint)])
    for sweep_index in range(1, SWEEPS):
        _, adjoint = sweep([adj_faces(adjoint)])

    state_elem = jnp.dot(prolong_elem, prim_elem, preferred_element_type=jnp.float32).astype(
        jnp.bfloat16
    )
    conv_in = jnp.dot(conv_grad, state_elem, preferred_element_type=jnp.float32)
    conv_flux = (state_elem * conv_in).astype(jnp.bfloat16)
    trace_jump = (own_rows - picked).astype(bf).reshape(4, elems, lanes)
    residual = jnp.dot(stiffness, state_elem, preferred_element_type=jnp.float32)
    residual = residual + jnp.dot(conv_out, conv_flux, preferred_element_type=jnp.float32)
    residual = (
        residual
        + jnp.einsum("vjr,jer->ve", lift_w, trace_jump, preferred_element_type=jnp.float32)
        - forcing.astype(jnp.float32)
    )
    measure = jnp.abs(jnp.sum(adjoint * residual, axis=0))
    alive = jnp.arange(measure.shape[0]) < elem_count[0]
    weighted = jnp.where(alive, elem_volume * measure, 0.0)
    totals = butterfly_sum(
        jnp.stack([jnp.sum(weighted), elem_count[0].astype(jnp.float32)])
    )
    mean_error = totals[0] / totals[1]
    return (weighted / mean_error, jnp.reshape(mean_error, (1,)))


def solution(mesh):
    placed = (
        P(None, AXES),
        P(None, AXES),
        P(None, AXES),
        P(AXES),
        P(None, AXES),
        P(AXES, None),
        P(AXES),
        P(),
        P(),
        P(),
        P(),
        P(),
        P(),
        P(),
        P(),
        P(),
        P(),
    )
    return jax.shard_map(
        local, mesh=mesh, in_specs=placed, out_specs=(P(AXES), P()), check_vma=False
    )
```

```python
import functools

import jax
import jax.numpy as jnp
from jax import lax
from jax.experimental import pallas as pl
from jax.experimental.pallas import tpu as pltpu
from jax.sharding import PartitionSpec as P

SWEEPS = 2
AXES = ("px", "py")


def _fill_pool(pool, parts):
    faces = parts[0].shape[0]
    chunk = 256

    def copy_own(i, carry):
        at = pl.multiple_of(i * chunk, chunk)
        total = parts[0][pl.ds(at, chunk), :].astype(jnp.float32)
        for part in parts[1:]:
            total = total + part[pl.ds(at, chunk), :].astype(jnp.float32)
        pool[pl.ds(at, chunk), :] = total
        return carry

    lax.fori_loop(0, faces // chunk, copy_own, 0)


def _gather_loop(idx_ref, pool, out_ref):
    def body(i, carry):
        row = idx_ref[i]
        out_ref[pl.ds(i, 1), :] = pool[pl.ds(row, 1), :]
        return carry

    lax.fori_loop(0, out_ref.shape[0], body, 0, unroll=16)


def _send_kernel(n_parts, idx_ref, *refs):
    parts, out_ref, pool = refs[:n_parts], refs[n_parts], refs[n_parts + 1]
    faces, width = parts[0].shape
    _fill_pool(pool, parts)
    pool[pl.ds(faces, 8), :] = jnp.zeros((8, width), jnp.float32)
    _gather_loop(idx_ref, pool, out_ref)


def _pull_kernel(n_parts, idx_ref, *refs):
    parts = refs[:n_parts]
    blocks = refs[n_parts : n_parts + 8]
    out_ref, pool = refs[n_parts + 8], refs[n_parts + 9]
    faces, width = parts[0].shape
    slots = blocks[0].shape[0]
    _fill_pool(pool, parts)
    for slot, block in zip((0, 1, 2, 3, 5, 6, 7, 8), blocks):
        pool[pl.ds(faces + slot * slots, slots), :] = block[...].astype(jnp.float32)
    pool[pl.ds(faces + 4 * slots, slots), :] = jnp.zeros((slots, width), jnp.float32)
    pool[pl.ds(faces + 9 * slots, 8), :] = jnp.zeros((8, width), jnp.float32)
    _gather_loop(idx_ref, pool, out_ref)


_VMEM = dict(compiler_params=pltpu.CompilerParams(vmem_limit_bytes=48 * 1024 * 1024))


def send_rows(parts, index):
    count, (faces, width) = index.shape[0], parts[0].shape
    return pl.pallas_call(
        functools.partial(_send_kernel, len(parts)),
        out_shape=jax.ShapeDtypeStruct((count, width), jnp.float32),
        in_specs=[pl.BlockSpec(memory_space=pltpu.SMEM)]
        + [pl.BlockSpec(memory_space=pltpu.VMEM)] * len(parts),
        out_specs=pl.BlockSpec(memory_space=pltpu.VMEM),
        scratch_shapes=[pltpu.VMEM((faces + 8, width), jnp.float32)],
        cost_estimate=pl.CostEstimate(
            flops=0, transcendentals=0, bytes_accessed=2 * count * width * 4
        ),
        **_VMEM,
    )(index, *parts)


def pull_rows(parts, blocks, index):
    count, (faces, width) = index.shape[0], parts[0].shape
    slots = blocks[0].shape[0]
    return pl.pallas_call(
        functools.partial(_pull_kernel, len(parts)),
        out_shape=jax.ShapeDtypeStruct((count, width), jnp.float32),
        in_specs=[pl.BlockSpec(memory_space=pltpu.SMEM)]
        + [pl.BlockSpec(memory_space=pltpu.VMEM)] * (len(parts) + len(blocks)),
        out_specs=pl.BlockSpec(memory_space=pltpu.VMEM),
        scratch_shapes=[pltpu.VMEM((faces + 9 * slots + 8, width), jnp.float32)],
        cost_estimate=pl.CostEstimate(
            flops=0, transcendentals=0, bytes_accessed=3 * count * width * 4
        ),
        **_VMEM,
    )(index, *parts, *blocks)


def exchange(parcel):
    n_px = lax.axis_size("px")
    n_py = lax.axis_size("py")
    blocks = [None] * 9
    for q in range(9):
        if q == 4:
            continue
        da, db = q // 3 - 1, q % 3 - 1
        pairs = []
        for r in range(n_px):
            for c in range(n_py):
                rr, cc = r + da, c + db
                if 0 <= rr < n_px and 0 <= cc < n_py:
                    pairs.append((r * n_py + c, rr * n_py + cc))
        blocks[8 - q] = lax.ppermute(parcel[q], AXES, pairs)
    return [blocks[t] for t in (0, 1, 2, 3, 5, 6, 7, 8)]


def butterfly_sum(value):
    n_py = lax.axis_size("py")
    total = lax.axis_size("px") * n_py
    bits = total.bit_length() - 1
    masks = [1 << b for b in range(bits)]
    for a, b in zip(masks[0::2], masks[1::2]):
        got = {}
        for m in (a, b, a ^ b):
            got[m] = lax.ppermute(value, AXES, [(i, i ^ m) for i in range(total)])
        value = (value + got[a]) + (got[b] + got[a ^ b])
    return value


def local(
    prim_elem,
    forcing,
    adj_source,
    elem_volume,
    face_link,
    send_map,
    elem_count,
    prolong_elem,
    face_trace,
    prolong_face,
    stiffness,
    conv_grad,
    conv_out,
    lift,
    adj_trace,
    adj_lift,
    block_corr,
):
    elems = face_link.shape[1]
    face_total = 4 * elems
    slot_total = send_map.shape[1]
    src_total = face_total + slot_total
    slot_row = jnp.clip(send_map[0], 0, face_total)
    link = jnp.clip(face_link.reshape(-1), 0, src_total)
    width = prolong_face.shape[0]

    lanes, half = 128, 64
    bf = jnp.bfloat16
    face_w = jnp.zeros((lanes, prolong_face.shape[1]), bf).at[:width].set(prolong_face)
    trace_w = jnp.zeros((4, lanes, adj_trace.shape[2]), bf).at[:, half : half + width].set(adj_trace)
    couple_w = jnp.zeros((adj_lift.shape[0], 4, lanes), bf).at[:, :, half : half + width].set(adj_lift)
    lift_w = jnp.zeros((lift.shape[0], 4, lanes), bf).at[:, :, :width].set(lift)

    coarse = jnp.einsum(
        "jrc,ce->jer", face_trace, prim_elem, preferred_element_type=jnp.float32
    ).astype(bf)
    own_rows = jnp.einsum(
        "jer,fr->jef", coarse, face_w, preferred_element_type=jnp.float32
    ).reshape(face_total, lanes)

    source = adj_source.astype(jnp.float32)
    adjoint = source + jnp.dot(block_corr, adj_source, preferred_element_type=jnp.float32)

    def adj_faces(adjoint):
        face_vals = jnp.einsum(
            "jrv,ve->jer", trace_w, adjoint.astype(bf), preferred_element_type=jnp.float32
        ).astype(bf)
        return face_vals.reshape(face_total, lanes)

    def sweep(parts):
        parcel = send_rows(parts, slot_row).astype(bf)
        blocks = exchange(parcel.reshape(9, -1, lanes))
        picked = pull_rows(parts, blocks, link)
        coupling = jnp.einsum(
            "vjr,jer->ve",
            couple_w,
            picked.astype(bf).reshape(4, elems, lanes),
            preferred_element_type=jnp.float32,
        )
        right_side = source - coupling
        adjoint = right_side + jnp.dot(
            block_corr, right_side.astype(bf), preferred_element_type=jnp.float32
        )
        return picked, adjoint, parcel

    picked, adjoint, _ = sweep([own_rows, adj_faces(adjoint)])
    for sweep_index in range(1, SWEEPS):
        _, adjoint, parcel = sweep([adj_faces(adjoint)])
        picked, _ = lax.optimization_barrier((picked, parcel))

    state_elem = jnp.dot(prolong_elem, prim_elem, preferred_element_type=jnp.float32).astype(
        jnp.bfloat16
    )
    conv_in = jnp.dot(conv_grad, state_elem, preferred_element_type=jnp.float32)
    conv_flux = (state_elem * conv_in).astype(jnp.bfloat16)
    trace_jump = (own_rows - picked).astype(bf).reshape(4, elems, lanes)
    residual = jnp.dot(stiffness, state_elem, preferred_element_type=jnp.float32)
    residual = residual + jnp.dot(conv_out, conv_flux, preferred_element_type=jnp.float32)
    residual = (
        residual
        + jnp.einsum("vjr,jer->ve", lift_w, trace_jump, preferred_element_type=jnp.float32)
        - forcing.astype(jnp.float32)
    )
    measure = jnp.abs(jnp.sum(adjoint * residual, axis=0))
    alive = jnp.arange(measure.shape[0]) < elem_count[0]
    weighted = jnp.where(alive, elem_volume * measure, 0.0)
    totals = butterfly_sum(
        jnp.stack([jnp.sum(weighted), elem_count[0].astype(jnp.float32)])
    )
    mean_error = totals[0] / totals[1]
    return (weighted / mean_error, jnp.reshape(mean_error, (1,)))


def solution(mesh):
    placed = (
        P(None, AXES),
        P(None, AXES),
        P(None, AXES),
        P(AXES),
        P(None, AXES),
        P(AXES, None),
        P(AXES),
        P(),
        P(),
        P(),
        P(),
        P(),
        P(),
        P(),
        P(),
        P(),
        P(),
    )
    return jax.shard_map(
        local, mesh=mesh, in_specs=placed, out_specs=(P(AXES), P()), check_vma=False
    )
```

```python
import jax
import jax.numpy as jnp
from jax import lax
from jax.experimental import pallas as pl
from jax.experimental.pallas import tpu as pltpu
from jax.sharding import PartitionSpec as P

SWEEPS = 2
AXES = ("px", "py")


def _send_kernel(idx_ref, own_ref, out_ref, pool):
    faces, width = own_ref.shape
    chunk = 256

    def copy_own(i, carry):
        at = pl.multiple_of(i * chunk, chunk)
        pool[pl.ds(at, chunk), :] = own_ref[pl.ds(at, chunk), :]
        return carry

    lax.fori_loop(0, faces // chunk, copy_own, 0)
    pool[pl.ds(faces, 8), :] = jnp.zeros((8, width), jnp.float32)

    def body(i, carry):
        row = idx_ref[i]
        out_ref[pl.ds(i, 1), :] = pool[pl.ds(row, 1), :]
        return carry

    lax.fori_loop(0, out_ref.shape[0], body, 0, unroll=32)


def _pull_kernel(idx_ref, own_ref, *refs):
    blocks, out_ref, pool = refs[:8], refs[8], refs[9]
    faces, width = own_ref.shape
    slots = blocks[0].shape[0]
    chunk = 256

    def copy_own(i, carry):
        at = pl.multiple_of(i * chunk, chunk)
        pool[pl.ds(at, chunk), :] = own_ref[pl.ds(at, chunk), :]
        return carry

    lax.fori_loop(0, faces // chunk, copy_own, 0)
    for slot, block in zip((0, 1, 2, 3, 5, 6, 7, 8), blocks):
        pool[pl.ds(faces + slot * slots, slots), :] = block[...].astype(jnp.float32)
    pool[pl.ds(faces + 4 * slots, slots), :] = jnp.zeros((slots, width), jnp.float32)
    pool[pl.ds(faces + 9 * slots, 8), :] = jnp.zeros((8, width), jnp.float32)

    def body(i, carry):
        row = idx_ref[i]
        out_ref[pl.ds(i, 1), :] = pool[pl.ds(row, 1), :]
        return carry

    lax.fori_loop(0, out_ref.shape[0], body, 0, unroll=32)


_VMEM = dict(compiler_params=pltpu.CompilerParams(vmem_limit_bytes=48 * 1024 * 1024))


def send_rows(own, index):
    count, width = index.shape[0], own.shape[1]
    return pl.pallas_call(
        _send_kernel,
        out_shape=jax.ShapeDtypeStruct((count, width), own.dtype),
        in_specs=[
            pl.BlockSpec(memory_space=pltpu.SMEM),
            pl.BlockSpec(memory_space=pltpu.VMEM),
        ],
        out_specs=pl.BlockSpec(memory_space=pltpu.VMEM),
        scratch_shapes=[pltpu.VMEM((own.shape[0] + 8, width), jnp.float32)],
        cost_estimate=pl.CostEstimate(
            flops=0, transcendentals=0, bytes_accessed=2 * count * width * 4
        ),
        **_VMEM,
    )(index, own)


def pull_rows(own, blocks, index):
    count, width = index.shape[0], own.shape[1]
    faces, slots = own.shape[0], blocks[0].shape[0]
    return pl.pallas_call(
        _pull_kernel,
        out_shape=jax.ShapeDtypeStruct((count, width), own.dtype),
        in_specs=[pl.BlockSpec(memory_space=pltpu.SMEM)]
        + [pl.BlockSpec(memory_space=pltpu.VMEM)] * (1 + len(blocks)),
        out_specs=pl.BlockSpec(memory_space=pltpu.VMEM),
        scratch_shapes=[pltpu.VMEM((faces + 9 * slots + 8, width), jnp.float32)],
        cost_estimate=pl.CostEstimate(
            flops=0, transcendentals=0, bytes_accessed=3 * count * width * 4
        ),
        **_VMEM,
    )(index, own, *blocks)


def exchange(parcel):
    n_px = lax.axis_size("px")
    n_py = lax.axis_size("py")
    blocks = [None] * 9
    for q in range(9):
        if q == 4:
            continue
        da, db = q // 3 - 1, q % 3 - 1
        pairs = []
        for r in range(n_px):
            for c in range(n_py):
                rr, cc = r + da, c + db
                if 0 <= rr < n_px and 0 <= cc < n_py:
                    pairs.append((r * n_py + c, rr * n_py + cc))
        blocks[8 - q] = lax.ppermute(parcel[q], AXES, pairs)
    return [blocks[t] for t in (0, 1, 2, 3, 5, 6, 7, 8)]


def butterfly_sum(value):
    n_py = lax.axis_size("py")
    total = lax.axis_size("px") * n_py
    bits = total.bit_length() - 1
    masks = [1 << b for b in range(bits)]
    for a, b in zip(masks[0::2], masks[1::2]):
        got = {}
        for m in (a, b, a ^ b):
            got[m] = lax.ppermute(value, AXES, [(i, i ^ m) for i in range(total)])
        value = (value + got[a]) + (got[b] + got[a ^ b])
    return value


def local(
    prim_elem,
    forcing,
    adj_source,
    elem_volume,
    face_link,
    send_map,
    elem_count,
    prolong_elem,
    face_trace,
    prolong_face,
    stiffness,
    conv_grad,
    conv_out,
    lift,
    adj_trace,
    adj_lift,
    block_corr,
):
    elems = face_link.shape[1]
    face_total = 4 * elems
    slot_total = send_map.shape[1]
    src_total = face_total + slot_total
    slot_row = jnp.clip(send_map[0], 0, face_total)
    link = jnp.clip(face_link.reshape(-1), 0, src_total)
    width = prolong_face.shape[0]

    lanes, half = 128, 64
    bf = jnp.bfloat16
    face_w = jnp.zeros((lanes, prolong_face.shape[1]), bf).at[:width].set(prolong_face)
    trace_w = jnp.zeros((4, lanes, adj_trace.shape[2]), bf).at[:, half : half + width].set(adj_trace)
    couple_w = jnp.zeros((adj_lift.shape[0], 4, lanes), bf).at[:, :, half : half + width].set(adj_lift)
    lift_w = jnp.zeros((lift.shape[0], 4, lanes), bf).at[:, :, :width].set(lift)

    coarse = jnp.einsum(
        "jrc,ce->jer", face_trace, prim_elem, preferred_element_type=jnp.float32
    ).astype(bf)
    own_rows = jnp.einsum(
        "jer,fr->jef", coarse, face_w, preferred_element_type=jnp.float32
    ).reshape(face_total, lanes)

    source = adj_source.astype(jnp.float32)
    adjoint = source + jnp.dot(block_corr, adj_source, preferred_element_type=jnp.float32)

    def adj_faces(adjoint):
        face_vals = jnp.einsum(
            "jrv,ve->jer", trace_w, adjoint.astype(bf), preferred_element_type=jnp.float32
        ).astype(bf)
        return face_vals.astype(jnp.float32).reshape(face_total, lanes)

    def sweep(rows):
        parcel = send_rows(rows, slot_row).astype(bf)
        blocks = exchange(parcel.reshape(9, -1, lanes))
        picked = pull_rows(rows, blocks, link)
        coupling = jnp.einsum(
            "vjr,jer->ve",
            couple_w,
            picked.astype(bf).reshape(4, elems, lanes),
            preferred_element_type=jnp.float32,
        )
        right_side = source - coupling
        adjoint = right_side + jnp.dot(
            block_corr, right_side.astype(bf), preferred_element_type=jnp.float32
        )
        return picked, adjoint

    picked, adjoint = sweep(own_rows + adj_faces(adjoint))
    for sweep_index in range(1, SWEEPS):
        _, adjoint = sweep(adj_faces(adjoint))

    state_elem = jnp.dot(prolong_elem, prim_elem, preferred_element_type=jnp.float32).astype(
        jnp.bfloat16
    )
    conv_in = jnp.dot(conv_grad, state_elem, preferred_element_type=jnp.float32)
    conv_flux = (state_elem * conv_in).astype(jnp.bfloat16)
    trace_jump = (own_rows - picked).astype(bf).reshape(4, elems, lanes)
    residual = jnp.dot(stiffness, state_elem, preferred_element_type=jnp.float32)
    residual = residual + jnp.dot(conv_out, conv_flux, preferred_element_type=jnp.float32)
    residual = (
        residual
        + jnp.einsum("vjr,jer->ve", lift_w, trace_jump, preferred_element_type=jnp.float32)
        - forcing.astype(jnp.float32)
    )
    measure = jnp.abs(jnp.sum(adjoint * residual, axis=0))
    alive = jnp.arange(measure.shape[0]) < elem_count[0]
    weighted = jnp.where(alive, elem_volume * measure, 0.0)
    totals = butterfly_sum(
        jnp.stack([jnp.sum(weighted), elem_count[0].astype(jnp.float32)])
    )
    mean_error = totals[0] / totals[1]
    return (weighted / mean_error, jnp.reshape(mean_error, (1,)))


def solution(mesh):
    placed = (
        P(None, AXES),
        P(None, AXES),
        P(None, AXES),
        P(AXES),
        P(None, AXES),
        P(AXES, None),
        P(AXES),
        P(),
        P(),
        P(),
        P(),
        P(),
        P(),
        P(),
        P(),
        P(),
        P(),
    )
    return jax.shard_map(
        local, mesh=mesh, in_specs=placed, out_specs=(P(AXES), P()), check_vma=False
    )
```

```python
import jax
import jax.numpy as jnp
from jax import lax
from jax.experimental import pallas as pl
from jax.experimental.pallas import tpu as pltpu
from jax.sharding import PartitionSpec as P

SWEEPS = 2
AXES = ("px", "py")


def _send_kernel(idx_ref, own_ref, out_ref, pool):
    faces, width = own_ref.shape
    chunk = 256

    def copy_own(i, carry):
        at = pl.multiple_of(i * chunk, chunk)
        pool[pl.ds(at, chunk), :] = own_ref[pl.ds(at, chunk), :]
        return carry

    lax.fori_loop(0, faces // chunk, copy_own, 0)
    pool[pl.ds(faces, 8), :] = jnp.zeros((8, width), jnp.float32)

    def body(i, carry):
        row = idx_ref[i]
        out_ref[pl.ds(i, 1), :] = pool[pl.ds(row, 1), :]
        return carry

    lax.fori_loop(0, out_ref.shape[0], body, 0, unroll=64)


def _pull_kernel(idx_ref, own_ref, *refs):
    blocks, out_ref, pool = refs[:8], refs[8], refs[9]
    faces, width = own_ref.shape
    slots = blocks[0].shape[0]
    chunk = 256

    def copy_own(i, carry):
        at = pl.multiple_of(i * chunk, chunk)
        pool[pl.ds(at, chunk), :] = own_ref[pl.ds(at, chunk), :]
        return carry

    lax.fori_loop(0, faces // chunk, copy_own, 0)
    for slot, block in zip((0, 1, 2, 3, 5, 6, 7, 8), blocks):
        pool[pl.ds(faces + slot * slots, slots), :] = block[...].astype(jnp.float32)
    pool[pl.ds(faces + 4 * slots, slots), :] = jnp.zeros((slots, width), jnp.float32)
    pool[pl.ds(faces + 9 * slots, 8), :] = jnp.zeros((8, width), jnp.float32)

    def body(i, carry):
        row = idx_ref[i]
        out_ref[pl.ds(i, 1), :] = pool[pl.ds(row, 1), :]
        return carry

    lax.fori_loop(0, out_ref.shape[0], body, 0, unroll=64)


_VMEM = dict(compiler_params=pltpu.CompilerParams(vmem_limit_bytes=48 * 1024 * 1024))


def send_rows(own, index):
    count, width = index.shape[0], own.shape[1]
    return pl.pallas_call(
        _send_kernel,
        out_shape=jax.ShapeDtypeStruct((count, width), own.dtype),
        in_specs=[
            pl.BlockSpec(memory_space=pltpu.SMEM),
            pl.BlockSpec(memory_space=pltpu.VMEM),
        ],
        out_specs=pl.BlockSpec(memory_space=pltpu.VMEM),
        scratch_shapes=[pltpu.VMEM((own.shape[0] + 8, width), jnp.float32)],
        cost_estimate=pl.CostEstimate(
            flops=0, transcendentals=0, bytes_accessed=2 * count * width * 4
        ),
        **_VMEM,
    )(index, own)


def pull_rows(own, blocks, index):
    count, width = index.shape[0], own.shape[1]
    faces, slots = own.shape[0], blocks[0].shape[0]
    return pl.pallas_call(
        _pull_kernel,
        out_shape=jax.ShapeDtypeStruct((count, width), own.dtype),
        in_specs=[pl.BlockSpec(memory_space=pltpu.SMEM)]
        + [pl.BlockSpec(memory_space=pltpu.VMEM)] * (1 + len(blocks)),
        out_specs=pl.BlockSpec(memory_space=pltpu.VMEM),
        scratch_shapes=[pltpu.VMEM((faces + 9 * slots + 8, width), jnp.float32)],
        cost_estimate=pl.CostEstimate(
            flops=0, transcendentals=0, bytes_accessed=3 * count * width * 4
        ),
        **_VMEM,
    )(index, own, *blocks)


def exchange(parcel):
    n_px = lax.axis_size("px")
    n_py = lax.axis_size("py")
    blocks = [None] * 9
    for q in range(9):
        if q == 4:
            continue
        da, db = q // 3 - 1, q % 3 - 1
        pairs = []
        for r in range(n_px):
            for c in range(n_py):
                rr, cc = r + da, c + db
                if 0 <= rr < n_px and 0 <= cc < n_py:
                    pairs.append((r * n_py + c, rr * n_py + cc))
        blocks[8 - q] = lax.ppermute(parcel[q], AXES, pairs)
    return [blocks[t] for t in (0, 1, 2, 3, 5, 6, 7, 8)]


def butterfly_sum(value):
    n_py = lax.axis_size("py")
    total = lax.axis_size("px") * n_py
    bits = total.bit_length() - 1
    masks = [1 << b for b in range(bits)]
    for a, b in zip(masks[0::2], masks[1::2]):
        got = {}
        for m in (a, b, a ^ b):
            got[m] = lax.ppermute(value, AXES, [(i, i ^ m) for i in range(total)])
        value = (value + got[a]) + (got[b] + got[a ^ b])
    return value


def local(
    prim_elem,
    forcing,
    adj_source,
    elem_volume,
    face_link,
    send_map,
    elem_count,
    prolong_elem,
    face_trace,
    prolong_face,
    stiffness,
    conv_grad,
    conv_out,
    lift,
    adj_trace,
    adj_lift,
    block_corr,
):
    elems = face_link.shape[1]
    face_total = 4 * elems
    slot_total = send_map.shape[1]
    src_total = face_total + slot_total
    slot_row = jnp.clip(send_map[0], 0, face_total)
    link = jnp.clip(face_link.reshape(-1), 0, src_total)
    width = prolong_face.shape[0]

    lanes, half = 128, 64
    bf = jnp.bfloat16
    face_w = jnp.zeros((lanes, prolong_face.shape[1]), bf).at[:width].set(prolong_face)
    trace_w = jnp.zeros((4, lanes, adj_trace.shape[2]), bf).at[:, half : half + width].set(adj_trace)
    couple_w = jnp.zeros((adj_lift.shape[0], 4, lanes), bf).at[:, :, half : half + width].set(adj_lift)
    lift_w = jnp.zeros((lift.shape[0], 4, lanes), bf).at[:, :, :width].set(lift)

    coarse = jnp.einsum(
        "jrc,ce->jer", face_trace, prim_elem, preferred_element_type=jnp.float32
    ).astype(bf)
    own_rows = jnp.einsum(
        "jer,fr->jef", coarse, face_w, preferred_element_type=jnp.float32
    ).reshape(face_total, lanes)

    source = adj_source.astype(jnp.float32)
    adjoint = source + jnp.dot(block_corr, adj_source, preferred_element_type=jnp.float32)

    def adj_faces(adjoint):
        face_vals = jnp.einsum(
            "jrv,ve->jer", trace_w, adjoint.astype(bf), preferred_element_type=jnp.float32
        ).astype(bf)
        return face_vals.astype(jnp.float32).reshape(face_total, lanes)

    def sweep(rows):
        parcel = send_rows(rows, slot_row).astype(bf)
        blocks = exchange(parcel.reshape(9, -1, lanes))
        picked = pull_rows(rows, blocks, link)
        coupling = jnp.einsum(
            "vjr,jer->ve",
            couple_w,
            picked.astype(bf).reshape(4, elems, lanes),
            preferred_element_type=jnp.float32,
        )
        right_side = source - coupling
        adjoint = right_side + jnp.dot(
            block_corr, right_side.astype(bf), preferred_element_type=jnp.float32
        )
        return picked, adjoint

    picked, adjoint = sweep(own_rows + adj_faces(adjoint))
    for sweep_index in range(1, SWEEPS):
        _, adjoint = sweep(adj_faces(adjoint))

    state_elem = jnp.dot(prolong_elem, prim_elem, preferred_element_type=jnp.float32).astype(
        jnp.bfloat16
    )
    conv_in = jnp.dot(conv_grad, state_elem, preferred_element_type=jnp.float32)
    conv_flux = (state_elem * conv_in).astype(jnp.bfloat16)
    trace_jump = (own_rows - picked).astype(bf).reshape(4, elems, lanes)
    residual = jnp.dot(stiffness, state_elem, preferred_element_type=jnp.float32)
    residual = residual + jnp.dot(conv_out, conv_flux, preferred_element_type=jnp.float32)
    residual = (
        residual
        + jnp.einsum("vjr,jer->ve", lift_w, trace_jump, preferred_element_type=jnp.float32)
        - forcing.astype(jnp.float32)
    )
    measure = jnp.abs(jnp.sum(adjoint * residual, axis=0))
    alive = jnp.arange(measure.shape[0]) < elem_count[0]
    weighted = jnp.where(alive, elem_volume * measure, 0.0)
    totals = butterfly_sum(
        jnp.stack([jnp.sum(weighted), elem_count[0].astype(jnp.float32)])
    )
    mean_error = totals[0] / totals[1]
    return (weighted / mean_error, jnp.reshape(mean_error, (1,)))


def solution(mesh):
    placed = (
        P(None, AXES),
        P(None, AXES),
        P(None, AXES),
        P(AXES),
        P(None, AXES),
        P(AXES, None),
        P(AXES),
        P(),
        P(),
        P(),
        P(),
        P(),
        P(),
        P(),
        P(),
        P(),
        P(),
    )
    return jax.shard_map(
        local, mesh=mesh, in_specs=placed, out_specs=(P(AXES), P()), check_vma=False
    )
```

```python
import jax
import jax.numpy as jnp
from jax import lax
from jax.experimental import pallas as pl
from jax.experimental.pallas import tpu as pltpu
from jax.sharding import PartitionSpec as P

SWEEPS = 2
AXES = ("px", "py")


def _send_kernel(idx_ref, own_ref, out_ref, pool):
    faces, width = own_ref.shape
    chunk = 256

    def copy_own(i, carry):
        at = pl.multiple_of(i * chunk, chunk)
        pool[pl.ds(at, chunk), :] = own_ref[pl.ds(at, chunk), :]
        return carry

    lax.fori_loop(0, faces // chunk, copy_own, 0, unroll=True)
    pool[pl.ds(faces, 8), :] = jnp.zeros((8, width), jnp.float32)

    def body(i, carry):
        row = idx_ref[i]
        out_ref[pl.ds(i, 1), :] = pool[pl.ds(row, 1), :]
        return carry

    lax.fori_loop(0, out_ref.shape[0], body, 0, unroll=128)


def _pull_kernel(idx_ref, own_ref, *refs):
    blocks, out_ref, pool = refs[:8], refs[8], refs[9]
    faces, width = own_ref.shape
    slots = blocks[0].shape[0]
    chunk = 256

    def copy_own(i, carry):
        at = pl.multiple_of(i * chunk, chunk)
        pool[pl.ds(at, chunk), :] = own_ref[pl.ds(at, chunk), :]
        return carry

    lax.fori_loop(0, faces // chunk, copy_own, 0, unroll=True)
    for slot, block in zip((0, 1, 2, 3, 5, 6, 7, 8), blocks):
        pool[pl.ds(faces + slot * slots, slots), :] = block[...].astype(jnp.float32)
    pool[pl.ds(faces + 4 * slots, slots), :] = jnp.zeros((slots, width), jnp.float32)
    pool[pl.ds(faces + 9 * slots, 8), :] = jnp.zeros((8, width), jnp.float32)

    def body(i, carry):
        row = idx_ref[i]
        out_ref[pl.ds(i, 1), :] = pool[pl.ds(row, 1), :]
        return carry

    lax.fori_loop(0, out_ref.shape[0], body, 0, unroll=128)


_VMEM = dict(compiler_params=pltpu.CompilerParams(vmem_limit_bytes=48 * 1024 * 1024))


def send_rows(own, index):
    count, width = index.shape[0], own.shape[1]
    return pl.pallas_call(
        _send_kernel,
        out_shape=jax.ShapeDtypeStruct((count, width), own.dtype),
        in_specs=[
            pl.BlockSpec(memory_space=pltpu.SMEM),
            pl.BlockSpec(memory_space=pltpu.VMEM),
        ],
        out_specs=pl.BlockSpec(memory_space=pltpu.VMEM),
        scratch_shapes=[pltpu.VMEM((own.shape[0] + 8, width), jnp.float32)],
        cost_estimate=pl.CostEstimate(
            flops=0, transcendentals=0, bytes_accessed=2 * count * width * 4
        ),
        **_VMEM,
    )(index, own)


def pull_rows(own, blocks, index):
    count, width = index.shape[0], own.shape[1]
    faces, slots = own.shape[0], blocks[0].shape[0]
    return pl.pallas_call(
        _pull_kernel,
        out_shape=jax.ShapeDtypeStruct((count, width), own.dtype),
        in_specs=[pl.BlockSpec(memory_space=pltpu.SMEM)]
        + [pl.BlockSpec(memory_space=pltpu.VMEM)] * (1 + len(blocks)),
        out_specs=pl.BlockSpec(memory_space=pltpu.VMEM),
        scratch_shapes=[pltpu.VMEM((faces + 9 * slots + 8, width), jnp.float32)],
        cost_estimate=pl.CostEstimate(
            flops=0, transcendentals=0, bytes_accessed=3 * count * width * 4
        ),
        **_VMEM,
    )(index, own, *blocks)


def exchange(parcel):
    n_px = lax.axis_size("px")
    n_py = lax.axis_size("py")
    blocks = [None] * 9
    for q in range(9):
        if q == 4:
            continue
        da, db = q // 3 - 1, q % 3 - 1
        pairs = []
        for r in range(n_px):
            for c in range(n_py):
                rr, cc = r + da, c + db
                if 0 <= rr < n_px and 0 <= cc < n_py:
                    pairs.append((r * n_py + c, rr * n_py + cc))
        blocks[8 - q] = lax.ppermute(parcel[q], AXES, pairs)
    return [blocks[t] for t in (0, 1, 2, 3, 5, 6, 7, 8)]


def butterfly_sum(value):
    n_py = lax.axis_size("py")
    total = lax.axis_size("px") * n_py
    bits = total.bit_length() - 1
    masks = [1 << b for b in range(bits)]
    for a, b in zip(masks[0::2], masks[1::2]):
        got = {}
        for m in (a, b, a ^ b):
            got[m] = lax.ppermute(value, AXES, [(i, i ^ m) for i in range(total)])
        value = (value + got[a]) + (got[b] + got[a ^ b])
    return value


def local(
    prim_elem,
    forcing,
    adj_source,
    elem_volume,
    face_link,
    send_map,
    elem_count,
    prolong_elem,
    face_trace,
    prolong_face,
    stiffness,
    conv_grad,
    conv_out,
    lift,
    adj_trace,
    adj_lift,
    block_corr,
):
    elems = face_link.shape[1]
    face_total = 4 * elems
    slot_total = send_map.shape[1]
    src_total = face_total + slot_total
    slot_row = jnp.clip(send_map[0], 0, face_total)
    link = jnp.clip(face_link.reshape(-1), 0, src_total)
    width = prolong_face.shape[0]

    lanes, half = 128, 64
    bf = jnp.bfloat16
    face_w = jnp.zeros((lanes, prolong_face.shape[1]), bf).at[:width].set(prolong_face)
    trace_w = jnp.zeros((4, lanes, adj_trace.shape[2]), bf).at[:, half : half + width].set(adj_trace)
    couple_w = jnp.zeros((adj_lift.shape[0], 4, lanes), bf).at[:, :, half : half + width].set(adj_lift)
    lift_w = jnp.zeros((lift.shape[0], 4, lanes), bf).at[:, :, :width].set(lift)

    coarse = jnp.einsum(
        "jrc,ce->jer", face_trace, prim_elem, preferred_element_type=jnp.float32
    ).astype(bf)
    own_rows = jnp.einsum(
        "jer,fr->jef", coarse, face_w, preferred_element_type=jnp.float32
    ).reshape(face_total, lanes)

    source = adj_source.astype(jnp.float32)
    adjoint = source + jnp.dot(block_corr, adj_source, preferred_element_type=jnp.float32)

    def adj_faces(adjoint):
        face_vals = jnp.einsum(
            "jrv,ve->jer", trace_w, adjoint.astype(bf), preferred_element_type=jnp.float32
        ).astype(bf)
        return face_vals.astype(jnp.float32).reshape(face_total, lanes)

    def sweep(rows):
        parcel = send_rows(rows, slot_row).astype(bf)
        blocks = exchange(parcel.reshape(9, -1, lanes))
        picked = pull_rows(rows, blocks, link)
        coupling = jnp.einsum(
            "vjr,jer->ve",
            couple_w,
            picked.astype(bf).reshape(4, elems, lanes),
            preferred_element_type=jnp.float32,
        )
        right_side = source - coupling
        adjoint = right_side + jnp.dot(
            block_corr, right_side.astype(bf), preferred_element_type=jnp.float32
        )
        return picked, adjoint

    picked, adjoint = sweep(own_rows + adj_faces(adjoint))
    for sweep_index in range(1, SWEEPS):
        _, adjoint = sweep(adj_faces(adjoint))

    state_elem = jnp.dot(prolong_elem, prim_elem, preferred_element_type=jnp.float32).astype(
        jnp.bfloat16
    )
    conv_in = jnp.dot(conv_grad, state_elem, preferred_element_type=jnp.float32)
    conv_flux = (state_elem * conv_in).astype(jnp.bfloat16)
    trace_jump = (own_rows - picked).astype(bf).reshape(4, elems, lanes)
    residual = jnp.dot(stiffness, state_elem, preferred_element_type=jnp.float32)
    residual = residual + jnp.dot(conv_out, conv_flux, preferred_element_type=jnp.float32)
    residual = (
        residual
        + jnp.einsum("vjr,jer->ve", lift_w, trace_jump, preferred_element_type=jnp.float32)
        - forcing.astype(jnp.float32)
    )
    measure = jnp.abs(jnp.sum(adjoint * residual, axis=0))
    alive = jnp.arange(measure.shape[0]) < elem_count[0]
    weighted = jnp.where(alive, elem_volume * measure, 0.0)
    totals = butterfly_sum(
        jnp.stack([jnp.sum(weighted), elem_count[0].astype(jnp.float32)])
    )
    mean_error = totals[0] / totals[1]
    return (weighted / mean_error, jnp.reshape(mean_error, (1,)))


def solution(mesh):
    placed = (
        P(None, AXES),
        P(None, AXES),
        P(None, AXES),
        P(AXES),
        P(None, AXES),
        P(AXES, None),
        P(AXES),
        P(),
        P(),
        P(),
        P(),
        P(),
        P(),
        P(),
        P(),
        P(),
        P(),
    )
    return jax.shard_map(
        local, mesh=mesh, in_specs=placed, out_specs=(P(AXES), P()), check_vma=False
    )
```

```python
import jax
import jax.numpy as jnp
from jax import lax
from jax.experimental import pallas as pl
from jax.experimental.pallas import tpu as pltpu
from jax.sharding import PartitionSpec as P

SWEEPS = 2
AXES = ("px", "py")


def _send_kernel(idx_ref, own_ref, out_ref, pool):
    faces, width = own_ref.shape
    chunk = 256

    def copy_own(i, carry):
        at = pl.multiple_of(i * chunk, chunk)
        pool[pl.ds(at, chunk), :] = own_ref[pl.ds(at, chunk), :]
        return carry

    lax.fori_loop(0, faces // chunk, copy_own, 0, unroll=True)
    pool[pl.ds(faces, 8), :] = jnp.zeros((8, width), jnp.float32)

    def body(i, carry):
        row = idx_ref[i]
        out_ref[pl.ds(i, 1), :] = pool[pl.ds(row, 1), :]
        return carry

    lax.fori_loop(0, out_ref.shape[0], body, 0, unroll=128)


def _pull_kernel(idx_ref, own_ref, *refs):
    blocks, out_ref, pool = refs[:8], refs[8], refs[9]
    faces, width = own_ref.shape
    slots = blocks[0].shape[0]
    chunk = 256

    def copy_own(i, carry):
        at = pl.multiple_of(i * chunk, chunk)
        pool[pl.ds(at, chunk), :] = own_ref[pl.ds(at, chunk), :]
        return carry

    lax.fori_loop(0, faces // chunk, copy_own, 0, unroll=True)
    for slot, block in zip((0, 1, 2, 3, 5, 6, 7, 8), blocks):
        pool[pl.ds(faces + slot * slots, slots), :] = block[...].astype(jnp.float32)
    pool[pl.ds(faces + 4 * slots, slots), :] = jnp.zeros((slots, width), jnp.float32)
    pool[pl.ds(faces + 9 * slots, 8), :] = jnp.zeros((8, width), jnp.float32)

    def body(i, carry):
        row = idx_ref[i]
        out_ref[pl.ds(i, 1), :] = pool[pl.ds(row, 1), :]
        return carry

    lax.fori_loop(0, out_ref.shape[0], body, 0, unroll=128)


_VMEM = dict(compiler_params=pltpu.CompilerParams(vmem_limit_bytes=48 * 1024 * 1024))


def send_rows(own, index):
    count, width = index.shape[0], own.shape[1]
    return pl.pallas_call(
        _send_kernel,
        out_shape=jax.ShapeDtypeStruct((count, width), own.dtype),
        in_specs=[
            pl.BlockSpec(memory_space=pltpu.SMEM),
            pl.BlockSpec(memory_space=pltpu.VMEM),
        ],
        out_specs=pl.BlockSpec(memory_space=pltpu.VMEM),
        scratch_shapes=[pltpu.VMEM((own.shape[0] + 8, width), jnp.float32)],
        cost_estimate=pl.CostEstimate(
            flops=0, transcendentals=0, bytes_accessed=2 * count * width * 4
        ),
        **_VMEM,
    )(index, own)


def pull_rows(own, blocks, index):
    count, width = index.shape[0], own.shape[1]
    faces, slots = own.shape[0], blocks[0].shape[0]
    return pl.pallas_call(
        _pull_kernel,
        out_shape=jax.ShapeDtypeStruct((count, width), own.dtype),
        in_specs=[pl.BlockSpec(memory_space=pltpu.SMEM)]
        + [pl.BlockSpec(memory_space=pltpu.VMEM)] * (1 + len(blocks)),
        out_specs=pl.BlockSpec(memory_space=pltpu.VMEM),
        scratch_shapes=[pltpu.VMEM((faces + 9 * slots + 8, width), jnp.float32)],
        cost_estimate=pl.CostEstimate(
            flops=0, transcendentals=0, bytes_accessed=3 * count * width * 4
        ),
        **_VMEM,
    )(index, own, *blocks)


def exchange(parcel):
    n_px = lax.axis_size("px")
    n_py = lax.axis_size("py")
    blocks = [None] * 9
    for q in range(9):
        if q == 4:
            continue
        da, db = q // 3 - 1, q % 3 - 1
        pairs = []
        for r in range(n_px):
            for c in range(n_py):
                rr, cc = r + da, c + db
                if 0 <= rr < n_px and 0 <= cc < n_py:
                    pairs.append((r * n_py + c, rr * n_py + cc))
        blocks[8 - q] = lax.ppermute(parcel[q], AXES, pairs)
    return [blocks[t] for t in (0, 1, 2, 3, 5, 6, 7, 8)]


def butterfly_sum(value):
    for axis in ("py", "px"):
        size = lax.axis_size(axis)
        step = 1
        while step < size:
            pairs = [(i, i ^ step) for i in range(size)]
            value = value + lax.ppermute(value, axis, pairs)
            step *= 2
    return value


def local(
    prim_elem,
    forcing,
    adj_source,
    elem_volume,
    face_link,
    send_map,
    elem_count,
    prolong_elem,
    face_trace,
    prolong_face,
    stiffness,
    conv_grad,
    conv_out,
    lift,
    adj_trace,
    adj_lift,
    block_corr,
):
    elems = face_link.shape[1]
    face_total = 4 * elems
    slot_total = send_map.shape[1]
    src_total = face_total + slot_total
    slot_row = jnp.clip(send_map[0], 0, face_total)
    link = jnp.clip(face_link.reshape(-1), 0, src_total)
    width = prolong_face.shape[0]

    lanes, half = 128, 64
    bf = jnp.bfloat16
    face_w = jnp.zeros((lanes, prolong_face.shape[1]), bf).at[:width].set(prolong_face)
    trace_w = jnp.zeros((4, lanes, adj_trace.shape[2]), bf).at[:, half : half + width].set(adj_trace)
    couple_w = jnp.zeros((adj_lift.shape[0], 4, lanes), bf).at[:, :, half : half + width].set(adj_lift)
    lift_w = jnp.zeros((lift.shape[0], 4, lanes), bf).at[:, :, :width].set(lift)

    coarse = jnp.einsum(
        "jrc,ce->jer", face_trace, prim_elem, preferred_element_type=jnp.float32
    ).astype(bf)
    own_rows = jnp.einsum(
        "jer,fr->jef", coarse, face_w, preferred_element_type=jnp.float32
    ).reshape(face_total, lanes)

    source = adj_source.astype(jnp.float32)
    adjoint = source + jnp.dot(block_corr, adj_source, preferred_element_type=jnp.float32)

    def adj_faces(adjoint):
        face_vals = jnp.einsum(
            "jrv,ve->jer", trace_w, adjoint.astype(bf), preferred_element_type=jnp.float32
        ).astype(bf)
        return face_vals.astype(jnp.float32).reshape(face_total, lanes)

    def sweep(rows):
        parcel = send_rows(rows, slot_row).astype(bf)
        blocks = exchange(parcel.reshape(9, -1, lanes))
        picked = pull_rows(rows, blocks, link)
        coupling = jnp.einsum(
            "vjr,jer->ve",
            couple_w,
            picked.astype(bf).reshape(4, elems, lanes),
            preferred_element_type=jnp.float32,
        )
        right_side = source - coupling
        adjoint = right_side + jnp.dot(
            block_corr, right_side.astype(bf), preferred_element_type=jnp.float32
        )
        return picked, adjoint

    picked, adjoint = sweep(own_rows + adj_faces(adjoint))
    for sweep_index in range(1, SWEEPS):
        _, adjoint = sweep(adj_faces(adjoint))

    state_elem = jnp.dot(prolong_elem, prim_elem, preferred_element_type=jnp.float32).astype(
        jnp.bfloat16
    )
    conv_in = jnp.dot(conv_grad, state_elem, preferred_element_type=jnp.float32)
    conv_flux = (state_elem * conv_in).astype(jnp.bfloat16)
    trace_jump = (own_rows - picked).astype(bf).reshape(4, elems, lanes)
    residual = jnp.dot(stiffness, state_elem, preferred_element_type=jnp.float32)
    residual = residual + jnp.dot(conv_out, conv_flux, preferred_element_type=jnp.float32)
    residual = (
        residual
        + jnp.einsum("vjr,jer->ve", lift_w, trace_jump, preferred_element_type=jnp.float32)
        - forcing.astype(jnp.float32)
    )
    measure = jnp.abs(jnp.sum(adjoint * residual, axis=0))
    alive = jnp.arange(measure.shape[0]) < elem_count[0]
    weighted = jnp.where(alive, elem_volume * measure, 0.0)
    totals = butterfly_sum(
        jnp.stack([jnp.sum(weighted), elem_count[0].astype(jnp.float32)])
    )
    mean_error = totals[0] / totals[1]
    return (weighted / mean_error, jnp.reshape(mean_error, (1,)))


def solution(mesh):
    placed = (
        P(None, AXES),
        P(None, AXES),
        P(None, AXES),
        P(AXES),
        P(None, AXES),
        P(AXES, None),
        P(AXES),
        P(),
        P(),
        P(),
        P(),
        P(),
        P(),
        P(),
        P(),
        P(),
        P(),
    )
    return jax.shard_map(
        local, mesh=mesh, in_specs=placed, out_specs=(P(AXES), P()), check_vma=False
    )
```
